128 devices in a mesh: shaft: 32 (over z, y, core), ply: 4 (over x).
Axes of the slice: x: 4, y: 4, z: 4, core: 2. Of those that a mesh axis runs over, the one named last changes fastest.
Arguments:
- displacement: float32 [64, 4, 8192], P(None, 'ply', 'shaft'), may hold values from -6 to 6
- velocity: float32 [64, 4, 8192], P(None, 'ply', 'shaft'), may hold values from -6 to 6
- external: float32 [64, 4, 8192], P(None, 'ply', 'shaft'), may hold values from -6 to 6
- mass_inverse: float32 [64, 4, 8192], P(None, 'ply', 'shaft'), may hold values from 0.5 to 2
- pattern: int32 [5, 4, 8192], P(None, 'ply', 'shaft'), may hold values from 0 to 8, as said below
- coupled: int32 [4, 8192], P('ply', 'shaft'), may hold values from 1 to 5
- stiffness_old: bfloat16 [5, 64, 64, 32768], P(None, None, None, ('shaft', 'ply')), may hold values from -0.3125 to 0.3125
- history_old: float32 [48, 32768], P(None, ('shaft', 'ply')), may hold values from -6 to 6
- decay_old: float32 [48, 32768], P(None, ('shaft', 'ply')), may hold values from 0.2 to 0.98
- strain_map: float32 [48, 64], replicated, may hold values from -0.75 to 0.75
- send_slot: int32 [128, 2, 32], P(('shaft', 'ply')), may hold values from 0 to 255, as said below
- arrive_place: int32 [128, 2, 32], P(('shaft', 'ply')), may hold values from 0 to 255, as said below
- arrive_count: int32 [128, 2], P(('shaft', 'ply')), may hold values from 0 to 32, as said below
Outputs:
- final_displacement: float32 [64, 4, 8192], P(None, 'ply', 'shaft')
- final_velocity: float32 [64, 4, 8192], P(None, 'ply', 'shaft')
- final_history: float32 [48, 4, 8192], P(None, 'ply', 'shaft')
The draws below stay inside these ranges and needn't reach their ends.
Inputs may be any that keep to these rules, and one draw needn't show every extreme that they name: pattern[0, q, s] is 4, the block itself; the codes of one block are distinct; code c names the block at ply offset c // 3 - 1 and shaft offset c % 3 - 1. coupled[q, s] counts the live entries of pattern[:, q, s]. send_slot[d, r, i] for i below the matching arrival count of the receiving neighbour is the old slot on d of the i-th block that moves from d toward neighbour r; entries past the count are 0; no slot of d is named twice. arrive_place[e, r, i] for i < arrive_count[e, r] is the new place on e of the i-th block arriving from neighbour r; these places are exactly the slots that e sends away, and all other blocks of e keep their slot; entries past the count are 0. `arrive_count`: as many blocks move from e to a neighbour as from that neighbour to e; counts toward a missing neighbour are 0.
All inputs are finite; a program needn't handle non-finite values.
Results may differ from the reference program's by a relative error of at most 0.00082.
Values may be sent and summed in bfloat16 or wider, within the bound.
No kernel may reach another device: no remote copies, remote signals or barrier semaphores. Data moves between devices by JAX's collectives and lax.ppermute only.
A program may use at most 192 MiB of HBM per device.

```python
import math
import jax
import jax.numpy as jnp
from jax import lax

NDOF = 64
NHIST = 48
PMAX = 5
ITERS = 4
CS = 256
RANKS = 128
CAP = 32
NPLY = 4
NS = 8192
NBLOCKS = 32768
N_SHAFT = 32
N_PLY = 4


def migration_plan(key):
    folded = jax.random.fold_in(key, 11)
    subkeys = jax.random.split(folded, 4)
    edges = jax.random.randint(subkeys[0], (N_SHAFT - 1, N_PLY), CAP // 2, CAP + 1).astype(jnp.int32)
    fullest_row = jax.random.randint(subkeys[1], (), 0, N_SHAFT - 1)
    fullest_col = jax.random.randint(subkeys[2], (), 0, N_PLY)
    hit = (jnp.arange(N_SHAFT - 1)[:, None] == fullest_row) & (jnp.arange(N_PLY)[None, :] == fullest_col)
    edges = jnp.where(hit, CAP, edges).astype(jnp.int32)
    empty = jnp.zeros((1, N_PLY), jnp.int32)
    lower = jnp.concatenate([empty, edges], 0).reshape(-1)
    upper = jnp.concatenate([edges, empty], 0).reshape(-1)
    orders = jax.vmap(lambda subkey: jax.random.permutation(subkey, CS))(jax.random.split(subkeys[3], RANKS)).astype(jnp.int32)
    offsets = jnp.arange(CAP, dtype=jnp.int32)[None, :]
    rows = jnp.arange(RANKS)[:, None]

    def pick(start, amount):
        entries = jnp.minimum(start[:, None] + offsets, CS - 1)
        return jnp.where(offsets < amount[:, None], orders[rows, entries], 0).astype(jnp.int32)
    zero = jnp.zeros((RANKS,), jnp.int32)
    sent = jnp.stack([pick(zero, lower), pick(lower, upper)], 1)
    places = jnp.stack([pick(upper, lower), pick(zero, upper)], 1)
    counts = jnp.stack([lower, upper], 1).astype(jnp.int32)
    return (sent, places, counts)


def draw_send_slot(key, part):
    return migration_plan(key)[0]


def draw_arrive_place(key, part):
    return migration_plan(key)[1]


def draw_arrive_count(key, part):
    return migration_plan(key)[2]


def draw_pattern(key, part):
    folded = jax.random.fold_in(key, 5)
    scores = jax.random.randint(folded, (NPLY, NS, 8), 0, 1 << 20) * 8 + jnp.arange(8)
    ranking = jnp.argsort(scores, axis=-1)[..., :PMAX - 1]
    others = jnp.array([0, 1, 2, 3, 5, 6, 7, 8], jnp.int32)[ranking]
    leading = jnp.full((NPLY, NS, 1), 4, jnp.int32)
    return jnp.moveaxis(jnp.concatenate([leading, others], -1), -1, 0).astype(jnp.int32)


def set_ends(values, rng, smallest, top_value):
    longest = values.shape.index(max(values.shape))
    spots = []
    for shift in (0, 1):
        where = [jax.random.randint(jax.random.fold_in(rng, axis), (), 0, length) for axis, length in enumerate(values.shape)]
        where[longest] = (where[longest] + shift) % values.shape[longest]
        spots.append(tuple(where))
    return values.at[spots[0]].set(smallest).at[spots[1]].set(top_value)


def level_of(own_key, extent, shards, least, top_value):
    def one(position, shards_of):
        draws = jax.random.uniform(jax.random.fold_in(jax.random.fold_in(own_key, 6), position), (shards_of,), jnp.float32, least / len(shards), top_value / len(shards))
        return jnp.repeat(jnp.exp(draws), extent[position] // shards_of).reshape((-1,) + (1,) * (len(extent) - position - 1))

    loudness = one(*shards[0])
    for cut in shards[1:]:
        loudness = loudness * one(*cut)
    return loudness


def normal_values(key, dims, scale, limit, pieces=(), kind=jnp.bfloat16):
    level = level_of(key, dims, pieces, -0.22, 0.18) if pieces else 1.0
    drawn = jax.random.normal(key, dims, jnp.float32) * scale * level
    return jnp.minimum(jnp.maximum(drawn, -limit), limit).astype(kind)


def setup_inputs(seed: int = 0) -> dict:
    streams_of = jax.random.split(jax.random.key(seed), 14)
    return {
        "displacement": normal_values(streams_of[0], (NDOF, NPLY, NS), 1.0, 6.0, ((1, 4), (2, 32)), jnp.float32),
        "velocity": normal_values(streams_of[1], (NDOF, NPLY, NS), 1.0, 6.0, ((1, 4), (2, 32)), jnp.float32),
        "external": normal_values(streams_of[2], (NDOF, NPLY, NS), 1.0, 6.0, ((1, 4), (2, 32)), jnp.float32),
        "mass_inverse": jnp.clip(jnp.exp(math.log(2.0) - 1.3862944 * jax.random.uniform(streams_of[3], (NDOF, NPLY, NS), jnp.float32) ** level_of(streams_of[3], (NDOF, NPLY, NS), ((1, 4), (2, 32)), -0.2, 0.2)), 0.5, 2.0),
        "pattern": draw_pattern(jax.random.fold_in(streams_of[13], 71), 0),
        "coupled": set_ends(jax.random.randint(streams_of[5], (NPLY, NS), 1, PMAX + 1), jax.random.fold_in(streams_of[5], 1), 1, PMAX).astype(jnp.int32),
        "stiffness_old": normal_values(streams_of[6], (PMAX, NDOF, NDOF, NBLOCKS), (NDOF * PMAX) ** -0.5, 0.3125, ((3, 128),)),
        "history_old": normal_values(streams_of[7], (NHIST, NBLOCKS), 1.0, 6.0, ((1, 128),), jnp.float32),
        "decay_old": jnp.clip(jnp.exp(math.log(0.98) - 1.5892352 * jax.random.uniform(streams_of[8], (NHIST, NBLOCKS), jnp.float32) ** level_of(streams_of[8], (NHIST, NBLOCKS), ((1, 128),), -0.2, 0.2)), 0.2, 0.98),
        "strain_map": normal_values(streams_of[9], (NHIST, NDOF), NDOF ** -0.5, 0.75, (), jnp.float32),
        "send_slot": draw_send_slot(jax.random.fold_in(streams_of[13], 71), 0),
        "arrive_place": draw_arrive_place(jax.random.fold_in(streams_of[13], 71), 0),
        "arrive_count": draw_arrive_count(jax.random.fold_in(streams_of[13], 71), 0),
    }


time_step = 0.25


def to_grid(flat):
    leading = flat.shape[:-1]
    cube = flat.reshape(leading + (N_SHAFT, N_PLY, CS))
    cube = jnp.moveaxis(cube, -2, -3)
    return cube.reshape(leading + (N_PLY, N_SHAFT * CS))


def source_lookup(send_slot, arrive_place, arrive_count):
    capacity = send_slot.shape[-1]
    receiver = jnp.arange(RANKS, dtype=jnp.int32)[:, None]
    lookup = jnp.arange(RANKS * CS + 1, dtype=jnp.int32)
    for side in range(2):
        sender = jnp.clip(receiver + (2 * side - 1) * N_PLY, 0, RANKS - 1).astype(jnp.int32)
        filled = jnp.arange(capacity, dtype=jnp.int32)[None, :] < arrive_count[:, side][:, None]
        target = jnp.where(filled, receiver * CS + arrive_place[:, side], RANKS * CS).astype(jnp.int32)
        anchor = (sender * CS + send_slot[sender[:, 0], 1 - side]).astype(jnp.int32)
        lookup = lookup.at[target.reshape(-1)].set(anchor.reshape(-1))
    return lookup[:RANKS * CS]


def reference(displacement, velocity, external, mass_inverse, pattern, coupled, stiffness_old, history_old, decay_old, strain_map, send_slot, arrive_place, arrive_count):
    lookup = source_lookup(send_slot, arrive_place, arrive_count)
    stiffness = to_grid(jnp.take(stiffness_old, lookup, axis=3))
    history = to_grid(jnp.take(history_old, lookup, axis=1))
    decay = to_grid(jnp.take(decay_old, lookup, axis=1))
    moved = displacement
    speeds = velocity
    for repeat in range(ITERS):
        rounded = moved.astype(jnp.bfloat16)
        padded = jnp.pad(rounded, ((0, 0), (1, 1), (1, 1)))
        force = jnp.zeros(moved.shape, jnp.float32)
        for slot_index in range(PMAX):
            picked = jnp.zeros_like(rounded)
            for code_index in range(9):
                ply_offset = code_index // 3
                shaft_offset = code_index % 3
                shifted = padded[:, ply_offset:ply_offset + NPLY, shaft_offset:shaft_offset + NS]
                picked = jnp.where(pattern[slot_index] == code_index, shifted, picked)
            picked = jnp.where(slot_index < coupled, picked, jnp.zeros_like(picked))
            force = force + jnp.einsum("ijqs,jqs->iqs", stiffness[slot_index].astype(jnp.float32), picked.astype(jnp.float32), precision=lax.Precision.HIGHEST)
        viscous = jnp.dot(strain_map.T, history.reshape(NHIST, -1), precision=lax.Precision.HIGHEST)
        force = force + viscous.reshape(moved.shape)
        speeds = speeds + time_step * (mass_inverse * (external - force))
        advanced = moved + time_step * speeds
        strain_step = jnp.dot(strain_map, (advanced - moved).reshape(NDOF, -1), precision=lax.Precision.HIGHEST)
        history = decay * history + strain_step.reshape(history.shape)
        moved = advanced
    return (moved, speeds, history)
```

```python
import jax
import jax.numpy as jnp
from jax import lax
from jax.sharding import PartitionSpec as P

ITERS = 4


time_step = 0.25


def padded_2(value, sides, width):
    for axis, dim in sides:
        size, length = (lax.axis_size(axis), value.shape[dim])
        up = [(i, (i + 1) % size) for i in range(size - 1)]
        down = [(j, i) for i, j in up]
        last = lax.slice_in_dim(value, length - width, length, axis=dim)
        first = lax.slice_in_dim(value, 0, width, axis=dim)
        before = lax.ppermute(last, axis, up)
        after = lax.ppermute(first, axis, down)
        value = jnp.concatenate([before, value, after], axis=dim)
    return value


def shaft_exchange(lower_bound, upper_bound):
    size = lax.axis_size("shaft")
    up = [(i, i + 1) for i in range(size - 1)]
    down = [(i + 1, i) for i in range(size - 1)]
    from_lower = lax.ppermute(upper_bound, "shaft", up)
    from_higher = lax.ppermute(lower_bound, "shaft", down)
    return from_lower, from_higher


def select_neighbours(padded, pattern, coupled):
    blocks = pattern.shape[-1]
    shifted = [
        padded[:, code_index // 3, code_index % 3 : code_index % 3 + blocks]
        for code_index in range(9)
    ]
    gathered = []
    for slot_index in range(pattern.shape[0]):
        picked = jnp.zeros_like(shifted[0])
        for code_index in range(9):
            picked = jnp.where(pattern[slot_index] == code_index, shifted[code_index], picked)
        gathered.append(jnp.where(slot_index < coupled, picked, jnp.zeros_like(picked)))
    return jnp.stack(gathered)


def block_force(stiffness, neighbours):
    product = stiffness.astype(jnp.float32) * neighbours.astype(jnp.float32)[:, None, :, :]
    return jnp.sum(product, axis=(0, 2))


def on_device(
    displacement,
    velocity,
    external,
    mass_inverse,
    pattern,
    coupled,
    stiffness_old,
    history_old,
    decay_old,
    strain_map,
    send_slot,
    arrive_place,
    arrive_count,
):
    blocks = displacement.shape[-1]
    capacity = send_slot.shape[2]
    outgoing = send_slot[0].reshape(-1)
    lanes = jnp.arange(blocks, dtype=jnp.int32)

    leaving = (lanes[:, None] == outgoing[None, :]).astype(jnp.bfloat16)
    stiff_out = jnp.einsum(
        "kijb,bm->kijm", stiffness_old, leaving, preferred_element_type=jnp.float32
    ).astype(jnp.bfloat16)
    stiff_lower, stiff_higher = shaft_exchange(
        stiff_out[..., :capacity], stiff_out[..., capacity:]
    )
    stiff_arrived = jnp.concatenate([stiff_lower, stiff_higher], -1)

    filled = (
        jnp.arange(capacity, dtype=jnp.int32)[None, :] < arrive_count[0][:, None]
    ).reshape(-1)
    places = arrive_place[0].reshape(-1)
    arriving = (lanes[:, None] == places[None, :]) & filled[None, :]
    is_arrival = jnp.any(arriving, axis=1)
    arriving_bf16 = arriving.astype(jnp.bfloat16)
    arriving_f32 = arriving.astype(jnp.float32)

    target = jnp.where(filled, places, blocks)
    placing = (
        jnp.arange(blocks + 1, dtype=jnp.int32)
        .at[target]
        .set(blocks + jnp.arange(2 * capacity, dtype=jnp.int32))[:blocks]
    )
    moving_state = jnp.concatenate(
        [jnp.take(history_old, outgoing, axis=1), jnp.take(decay_old, outgoing, axis=1)], 0
    )
    state_lower, state_higher = shaft_exchange(
        moving_state[:, :capacity], moving_state[:, capacity:]
    )
    state_arrived = jnp.concatenate([state_lower, state_higher], 1)
    depth = history_old.shape[0]
    history = jnp.take(jnp.concatenate([history_old, state_arrived[:depth]], 1), placing, axis=1)
    decay = jnp.take(jnp.concatenate([decay_old, state_arrived[depth:]], 1), placing, axis=1)

    moved = displacement[:, 0, :]
    speeds = velocity[:, 0, :]
    forcing = external[:, 0, :]
    scaling = mass_inverse[:, 0, :]
    codes = pattern[:, 0, :]
    live_count = coupled[0]
    for repeat in range(ITERS):
        rounded = moved.astype(jnp.bfloat16)[:, None, :]
        padded = padded_2(rounded, (("shaft", 2), ("ply", 1)), 1)
        neighbours = select_neighbours(padded, codes, live_count)
        force_old = block_force(stiffness_old, neighbours)
        neighbours_arrived = jnp.einsum(
            "kjb,bm->kjm", neighbours, arriving_bf16, preferred_element_type=jnp.float32
        ).astype(jnp.bfloat16)
        force_arrived = block_force(stiff_arrived, neighbours_arrived)
        force_placed = jnp.dot(
            force_arrived, arriving_f32.T, precision=lax.Precision.HIGHEST
        )
        force = jnp.where(is_arrival[None, :], force_placed, force_old) + jnp.dot(
            strain_map.T, history, precision=lax.Precision.HIGHEST
        )
        speeds = speeds + time_step * (scaling * (forcing - force))
        advanced = moved + time_step * speeds
        history = decay * history + jnp.dot(
            strain_map, advanced - moved, precision=lax.Precision.HIGHEST
        )
        moved = advanced
    return (moved[:, None, :], speeds[:, None, :], history[:, None, :])


def solution(mesh):
    in_specs = (
        P(None, "ply", "shaft"),
        P(None, "ply", "shaft"),
        P(None, "ply", "shaft"),
        P(None, "ply", "shaft"),
        P(None, "ply", "shaft"),
        P("ply", "shaft"),
        P(None, None, None, ("shaft", "ply")),
        P(None, ("shaft", "ply")),
        P(None, ("shaft", "ply")),
        P(),
        P(("shaft", "ply"), None, None),
        P(("shaft", "ply"), None, None),
        P(("shaft", "ply"), None),
    )
    out_specs = (P(None, "ply", "shaft"), P(None, "ply", "shaft"), P(None, "ply", "shaft"))
    return jax.shard_map(
        on_device, mesh=mesh, in_specs=in_specs, out_specs=out_specs, check_vma=False
    )
```

```python
import jax
import jax.numpy as jnp
from jax import lax
from jax.sharding import PartitionSpec as P

ITERS = 4


time_step = 0.25


def neighbour_exchange(axis, lower_bound, upper_bound):
    size = lax.axis_size(axis)
    up = [(i, i + 1) for i in range(size - 1)]
    down = [(i + 1, i) for i in range(size - 1)]
    from_lower = lax.ppermute(upper_bound, axis, up)
    from_higher = lax.ppermute(lower_bound, axis, down)
    return from_lower, from_higher


def block_force(stiffness, neighbours):
    product = None
    for slot_index, picked in enumerate(neighbours):
        term = stiffness[slot_index].astype(jnp.float32) * picked.astype(jnp.float32)[None, :, :]
        product = term if product is None else product + term
    return jnp.sum(product, axis=1)


def on_device(
    displacement,
    velocity,
    external,
    mass_inverse,
    pattern,
    coupled,
    stiffness_old,
    history_old,
    decay_old,
    strain_map,
    send_slot,
    arrive_place,
    arrive_count,
):
    blocks = displacement.shape[-1]
    capacity = send_slot.shape[2]
    slots, rows_i, rows_j, _ = stiffness_old.shape
    outgoing = send_slot[0].reshape(-1)
    lanes = jnp.arange(blocks, dtype=jnp.int32)

    leaving = (lanes[:, None] == outgoing[None, :]).astype(jnp.bfloat16)
    stiff_out = (
        jnp.dot(
            stiffness_old.reshape(slots * rows_i * rows_j, blocks),
            leaving,
            preferred_element_type=jnp.float32,
        )
        .astype(jnp.bfloat16)
        .reshape(slots, rows_i, rows_j, 2 * capacity)
    )
    stiff_lower, stiff_higher = neighbour_exchange(
        "shaft", stiff_out[..., :capacity], stiff_out[..., capacity:]
    )
    stiff_arrived = jnp.concatenate([stiff_lower, stiff_higher], -1)

    filled = (
        jnp.arange(capacity, dtype=jnp.int32)[None, :] < arrive_count[0][:, None]
    ).reshape(-1)
    places = arrive_place[0].reshape(-1)
    arriving = (lanes[:, None] == places[None, :]) & filled[None, :]
    is_arrival = jnp.any(arriving, axis=1)
    arriving_bf16 = arriving.astype(jnp.bfloat16)
    arriving_f32 = arriving.astype(jnp.float32)

    edge_pick = jnp.stack([arriving_bf16[0], arriving_bf16[blocks - 1]], 1)
    stiff_edge_arrived = jnp.einsum(
        "kijm,me->kije", stiff_arrived, edge_pick, preferred_element_type=jnp.float32
    ).astype(jnp.bfloat16)
    stiff_edge_old = jnp.concatenate(
        [stiffness_old[..., :1], stiffness_old[..., blocks - 1 :]], -1
    )
    edge_arrival = jnp.stack([is_arrival[0], is_arrival[blocks - 1]])
    stiff_edge = jnp.where(edge_arrival, stiff_edge_arrived, stiff_edge_old)

    target = jnp.where(filled, places, blocks)
    placing = (
        jnp.arange(blocks + 1, dtype=jnp.int32)
        .at[target]
        .set(blocks + jnp.arange(2 * capacity, dtype=jnp.int32))[:blocks]
    )
    moving_state = jnp.concatenate(
        [jnp.take(history_old, outgoing, axis=1), jnp.take(decay_old, outgoing, axis=1)], 0
    )
    state_lower, state_higher = neighbour_exchange(
        "shaft", moving_state[:, :capacity], moving_state[:, capacity:]
    )
    state_arrived = jnp.concatenate([state_lower, state_higher], 1)
    depth = history_old.shape[0]
    history = jnp.take(jnp.concatenate([history_old, state_arrived[:depth]], 1), placing, axis=1)
    decay = jnp.take(jnp.concatenate([decay_old, state_arrived[depth:]], 1), placing, axis=1)

    moved = displacement[:, 0, :]
    speeds = velocity[:, 0, :]
    forcing = external[:, 0, :]
    scaling = mass_inverse[:, 0, :]
    live = jnp.arange(slots, dtype=jnp.int32)[:, None] < coupled[0][None, :]
    codes = jnp.where(live, pattern[:, 0, :], 9)
    halo_rows = jnp.arange(3, dtype=jnp.int32)[None, :] * 3
    reads_low = codes[:, :1] == halo_rows
    reads_high = codes[:, blocks - 1 :] == halo_rows + 2
    first_lane = (lanes == 0)[None, :]
    last_lane = (lanes == blocks - 1)[None, :]
    for repeat in range(ITERS):
        rounded = moved.astype(jnp.bfloat16)
        row_low, row_high = neighbour_exchange("ply", rounded, rounded)
        force_self = jnp.sum(
            stiffness_old[0].astype(jnp.float32) * rounded.astype(jnp.float32)[None, :, :], axis=1
        )
        viscous = jnp.dot(strain_map.T, history, precision=lax.Precision.HIGHEST)
        rows = (row_low, rounded, row_high)
        edge_first = jnp.stack([r[:, 0] for r in rows], 1)
        edge_last = jnp.stack([r[:, blocks - 1] for r in rows], 1)
        halo_low, halo_high = neighbour_exchange("shaft", edge_first, edge_last)

        shifted = []
        for code_index in range(9):
            r = rows[code_index // 3]
            offset = code_index % 3
            if offset == 0:
                shifted.append(jnp.pad(r[:, : blocks - 1], ((0, 0), (1, 0))))
            elif offset == 1:
                shifted.append(r)
            else:
                shifted.append(jnp.pad(r[:, 1:], ((0, 0), (0, 1))))
        neighbours = [rounded]
        for slot_index in range(1, slots):
            picked = jnp.zeros_like(rounded)
            for code_index in range(9):
                picked = jnp.where(codes[slot_index] == code_index, shifted[code_index], picked)
            neighbours.append(picked)
        force_rest = block_force(stiffness_old[1:], neighbours[1:])
        neighbours_arrived = [
            jnp.dot(picked, arriving_bf16, preferred_element_type=jnp.float32).astype(jnp.bfloat16)
            for picked in neighbours
        ]
        force_arrived = block_force(stiff_arrived, neighbours_arrived)
        force_placed = jnp.dot(force_arrived, arriving_f32.T, precision=lax.Precision.HIGHEST)

        delta_low = jnp.zeros((slots, rows_j), jnp.float32)
        delta_high = jnp.zeros((slots, rows_j), jnp.float32)
        for r in range(3):
            delta_low = jnp.where(
                reads_low[:, r : r + 1], halo_low[None, :, r].astype(jnp.float32), delta_low
            )
            delta_high = jnp.where(
                reads_high[:, r : r + 1], halo_high[None, :, r].astype(jnp.float32), delta_high
            )
        fix_low = jnp.sum(stiff_edge[..., 0].astype(jnp.float32) * delta_low[:, None, :], axis=(0, 2))
        fix_high = jnp.sum(
            stiff_edge[..., 1].astype(jnp.float32) * delta_high[:, None, :], axis=(0, 2)
        )

        force = (
            jnp.where(is_arrival[None, :], force_placed, force_self + force_rest)
            + jnp.where(first_lane, fix_low[:, None], 0.0)
            + jnp.where(last_lane, fix_high[:, None], 0.0)
            + viscous
        )
        speeds = speeds + time_step * (scaling * (forcing - force))
        advanced = moved + time_step * speeds
        history = decay * history + jnp.dot(
            strain_map, advanced - moved, precision=lax.Precision.HIGHEST
        )
        moved = advanced
    return (moved[:, None, :], speeds[:, None, :], history[:, None, :])


def solution(mesh):
    in_specs = (
        P(None, "ply", "shaft"),
        P(None, "ply", "shaft"),
        P(None, "ply", "shaft"),
        P(None, "ply", "shaft"),
        P(None, "ply", "shaft"),
        P("ply", "shaft"),
        P(None, None, None, ("shaft", "ply")),
        P(None, ("shaft", "ply")),
        P(None, ("shaft", "ply")),
        P(),
        P(("shaft", "ply"), None, None),
        P(("shaft", "ply"), None, None),
        P(("shaft", "ply"), None),
    )
    out_specs = (P(None, "ply", "shaft"), P(None, "ply", "shaft"), P(None, "ply", "shaft"))
    return jax.shard_map(
        on_device, mesh=mesh, in_specs=in_specs, out_specs=out_specs, check_vma=False
    )
```

```python
import jax
import jax.numpy as jnp
from jax import lax
from jax.experimental import pallas as pl
from jax.experimental.pallas import tpu as pltpu
from jax.sharding import PartitionSpec as P

ITERS = 4
ROWS = 8


time_step = 0.25


def padded_2(value, sides, width):
    for axis, dim in sides:
        size, length = (lax.axis_size(axis), value.shape[dim])
        up = [(i, (i + 1) % size) for i in range(size - 1)]
        down = [(j, i) for i, j in up]
        last = lax.slice_in_dim(value, length - width, length, axis=dim)
        first = lax.slice_in_dim(value, 0, width, axis=dim)
        before = lax.ppermute(last, axis, up)
        after = lax.ppermute(first, axis, down)
        value = jnp.concatenate([before, value, after], axis=dim)
    return value


def neighbour_exchange(axis, lower_bound, upper_bound):
    size = lax.axis_size(axis)
    up = [(i, i + 1) for i in range(size - 1)]
    down = [(i + 1, i) for i in range(size - 1)]
    from_lower = lax.ppermute(upper_bound, axis, up)
    from_higher = lax.ppermute(lower_bound, axis, down)
    return from_lower, from_higher


def gather_kernel(s_ref, lo_ref, hi_ref, out_lo_ref, out_hi_ref):
    rows, depth, blocks = s_ref.shape[1:]
    flat = s_ref[0].reshape(rows * depth, blocks)
    for pick_ref, out_ref in ((lo_ref, out_lo_ref), (hi_ref, out_hi_ref)):
        picked = jnp.dot(flat, pick_ref[...], preferred_element_type=jnp.float32)
        out_ref[0] = picked.reshape(rows, depth, -1).astype(out_ref.dtype)


def gather_leaving(stiffness, pick_lo, pick_hi):
    slots, rows_i, rows_j, blocks = stiffness.shape
    width = pick_lo.shape[1]
    out = jax.ShapeDtypeStruct((slots, rows_i, rows_j, width), stiffness.dtype)
    return pl.pallas_call(
        gather_kernel,
        grid=(slots, rows_i // ROWS),
        in_specs=[
            pl.BlockSpec((1, ROWS, rows_j, blocks), lambda k, i: (k, i, 0, 0)),
            pl.BlockSpec((blocks, width), lambda k, i: (0, 0)),
            pl.BlockSpec((blocks, width), lambda k, i: (0, 0)),
        ],
        out_specs=[
            pl.BlockSpec((1, ROWS, rows_j, width), lambda k, i: (k, i, 0, 0)),
            pl.BlockSpec((1, ROWS, rows_j, width), lambda k, i: (k, i, 0, 0)),
        ],
        out_shape=[out, out],
    )(stiffness, pick_lo, pick_hi)


def merge_kernel(s_ref, lo_ref, hi_ref, place_lo_ref, place_hi_ref, arrival_ref, out_ref):
    rows, depth, blocks = s_ref.shape[1:]
    width = lo_ref.shape[-1]
    placed = jnp.dot(
        lo_ref[0].reshape(rows * depth, width), place_lo_ref[...],
        preferred_element_type=jnp.float32,
    ) + jnp.dot(
        hi_ref[0].reshape(rows * depth, width), place_hi_ref[...],
        preferred_element_type=jnp.float32,
    )
    placed = placed.reshape(rows, depth, blocks).astype(out_ref.dtype)
    out_ref[0] = jnp.where(arrival_ref[...] > 0, placed, s_ref[0])


def merge_arrived(stiffness, arrived_lo, arrived_hi, place_lo, place_hi, arrival):
    slots, rows_i, rows_j, blocks = stiffness.shape
    width = arrived_lo.shape[-1]
    return pl.pallas_call(
        merge_kernel,
        grid=(slots, rows_i // ROWS),
        in_specs=[
            pl.BlockSpec((1, ROWS, rows_j, blocks), lambda k, i: (k, i, 0, 0)),
            pl.BlockSpec((1, ROWS, rows_j, width), lambda k, i: (k, i, 0, 0)),
            pl.BlockSpec((1, ROWS, rows_j, width), lambda k, i: (k, i, 0, 0)),
            pl.BlockSpec((width, blocks), lambda k, i: (0, 0)),
            pl.BlockSpec((width, blocks), lambda k, i: (0, 0)),
            pl.BlockSpec((1, blocks), lambda k, i: (0, 0)),
        ],
        out_specs=pl.BlockSpec((1, ROWS, rows_j, blocks), lambda k, i: (k, i, 0, 0)),
        out_shape=jax.ShapeDtypeStruct(stiffness.shape, stiffness.dtype),
    )(stiffness, arrived_lo, arrived_hi, place_lo, place_hi, arrival)


def force_kernel(s_ref, n_ref, out_ref):
    slots, rows = s_ref.shape[:2]
    for row in range(rows):
        acc = s_ref[0, row].astype(jnp.float32) * n_ref[0]
        for slot_index in range(1, slots):
            acc = acc + s_ref[slot_index, row].astype(jnp.float32) * n_ref[slot_index]
        out_ref[pl.ds(row, 1), :] = jnp.sum(acc, axis=0, keepdims=True)


def block_force(stiffness, neighbours):
    slots, rows_i, rows_j, blocks = stiffness.shape
    return pl.pallas_call(
        force_kernel,
        grid=(rows_i // ROWS,),
        in_specs=[
            pl.BlockSpec((slots, ROWS, rows_j, blocks), lambda i: (0, i, 0, 0)),
            pl.BlockSpec((slots, rows_j, blocks), lambda i: (0, 0, 0)),
        ],
        out_specs=pl.BlockSpec((ROWS, blocks), lambda i: (i, 0)),
        out_shape=jax.ShapeDtypeStruct((rows_i, blocks), jnp.float32),
        cost_estimate=pl.CostEstimate(
            flops=2 * slots * rows_i * rows_j * blocks,
            bytes_accessed=stiffness.size * 2 + neighbours.size * 4 + rows_i * blocks * 4,
            transcendentals=0,
        ),
    )(stiffness, neighbours)


def on_device(
    displacement,
    velocity,
    external,
    mass_inverse,
    pattern,
    coupled,
    stiffness_old,
    history_old,
    decay_old,
    strain_map,
    send_slot,
    arrive_place,
    arrive_count,
):
    blocks = displacement.shape[-1]
    capacity = send_slot.shape[2]
    slots = stiffness_old.shape[0]
    lanes = jnp.arange(blocks, dtype=jnp.int32)

    leave_lo = (lanes[:, None] == send_slot[0, 0][None, :]).astype(jnp.bfloat16)
    leave_hi = (lanes[:, None] == send_slot[0, 1][None, :]).astype(jnp.bfloat16)
    stiff_to_lower, stiff_to_higher = gather_leaving(stiffness_old, leave_lo, leave_hi)
    stiff_lower, stiff_higher = neighbour_exchange("shaft", stiff_to_lower, stiff_to_higher)

    count_live = jnp.arange(capacity, dtype=jnp.int32)[None, :] < arrive_count[0][:, None]
    place_lo = (arrive_place[0, 0][:, None] == lanes[None, :]) & count_live[0][:, None]
    place_hi = (arrive_place[0, 1][:, None] == lanes[None, :]) & count_live[1][:, None]
    arrival = (jnp.any(place_lo, 0) | jnp.any(place_hi, 0)).astype(jnp.int32)[None, :]
    stiffness = merge_arrived(
        stiffness_old,
        stiff_lower,
        stiff_higher,
        place_lo.astype(jnp.bfloat16),
        place_hi.astype(jnp.bfloat16),
        arrival,
    )

    outgoing = send_slot[0].reshape(-1)
    filled = count_live.reshape(-1)
    target = jnp.where(filled, arrive_place[0].reshape(-1), blocks)
    placing = (
        jnp.arange(blocks + 1, dtype=jnp.int32)
        .at[target]
        .set(blocks + jnp.arange(2 * capacity, dtype=jnp.int32))[:blocks]
    )
    moving_state = jnp.concatenate(
        [jnp.take(history_old, outgoing, axis=1), jnp.take(decay_old, outgoing, axis=1)], 0
    )
    state_lower, state_higher = neighbour_exchange(
        "shaft", moving_state[:, :capacity], moving_state[:, capacity:]
    )
    state_arrived = jnp.concatenate([state_lower, state_higher], 1)
    depth = history_old.shape[0]
    history = jnp.take(jnp.concatenate([history_old, state_arrived[:depth]], 1), placing, axis=1)
    decay = jnp.take(jnp.concatenate([decay_old, state_arrived[depth:]], 1), placing, axis=1)

    moved = displacement[:, 0, :]
    speeds = velocity[:, 0, :]
    forcing = external[:, 0, :]
    scaling = mass_inverse[:, 0, :]
    live = jnp.arange(slots, dtype=jnp.int32)[:, None] < coupled[0][None, :]
    codes = jnp.where(live, pattern[:, 0, :], 9)[:, None, :]
    for repeat in range(ITERS):
        rounded = moved.astype(jnp.bfloat16)[:, None, :]
        padded = padded_2(rounded, (("shaft", 2), ("ply", 1)), 1)
        neighbours = jnp.zeros((slots,) + moved.shape, jnp.float32)
        for code_index in range(9):
            shifted = padded[:, code_index // 3, code_index % 3 : code_index % 3 + blocks]
            neighbours = jnp.where(
                codes == code_index, shifted.astype(jnp.float32)[None], neighbours
            )
        force = block_force(stiffness, neighbours) + jnp.dot(
            strain_map.T, history, precision=lax.Precision.HIGHEST
        )
        speeds = speeds + time_step * (scaling * (forcing - force))
        advanced = moved + time_step * speeds
        history = decay * history + jnp.dot(
            strain_map, advanced - moved, precision=lax.Precision.HIGHEST
        )
        moved = advanced
    return (moved[:, None, :], speeds[:, None, :], history[:, None, :])


def solution(mesh):
    in_specs = (
        P(None, "ply", "shaft"),
        P(None, "ply", "shaft"),
        P(None, "ply", "shaft"),
        P(None, "ply", "shaft"),
        P(None, "ply", "shaft"),
        P("ply", "shaft"),
        P(None, None, None, ("shaft", "ply")),
        P(None, ("shaft", "ply")),
        P(None, ("shaft", "ply")),
        P(),
        P(("shaft", "ply"), None, None),
        P(("shaft", "ply"), None, None),
        P(("shaft", "ply"), None),
    )
    out_specs = (P(None, "ply", "shaft"), P(None, "ply", "shaft"), P(None, "ply", "shaft"))
    return jax.shard_map(
        on_device, mesh=mesh, in_specs=in_specs, out_specs=out_specs, check_vma=False
    )
```

```python
import jax
import jax.numpy as jnp
from jax import lax
from jax.experimental import pallas as pl
from jax.experimental.pallas import tpu as pltpu
from jax.sharding import PartitionSpec as P

ITERS = 4
ROWS = 8


time_step = 0.25


def padded_2(value, sides, width):
    for axis, dim in sides:
        size, length = (lax.axis_size(axis), value.shape[dim])
        up = [(i, (i + 1) % size) for i in range(size - 1)]
        down = [(j, i) for i, j in up]
        last = lax.slice_in_dim(value, length - width, length, axis=dim)
        first = lax.slice_in_dim(value, 0, width, axis=dim)
        before = lax.ppermute(last, axis, up)
        after = lax.ppermute(first, axis, down)
        value = jnp.concatenate([before, value, after], axis=dim)
    return value


def neighbour_exchange(axis, lower_bound, upper_bound):
    size = lax.axis_size(axis)
    up = [(i, i + 1) for i in range(size - 1)]
    down = [(i + 1, i) for i in range(size - 1)]
    from_lower = lax.ppermute(upper_bound, axis, up)
    from_higher = lax.ppermute(lower_bound, axis, down)
    return from_lower, from_higher


def gather_kernel(s_ref, lo_ref, hi_ref, out_lo_ref, out_hi_ref):
    rows, depth, blocks = s_ref.shape[1:]
    flat = s_ref[0].reshape(rows * depth, blocks)
    for pick_ref, out_ref in ((lo_ref, out_lo_ref), (hi_ref, out_hi_ref)):
        picked = jnp.dot(flat, pick_ref[...], preferred_element_type=jnp.float32)
        out_ref[0] = picked.reshape(rows, depth, -1).astype(out_ref.dtype)


def gather_leaving(stiffness, pick_lo, pick_hi):
    slots, rows_i, rows_j, blocks = stiffness.shape
    width = pick_lo.shape[1]
    out = jax.ShapeDtypeStruct((slots, rows_i, rows_j, width), stiffness.dtype)
    return pl.pallas_call(
        gather_kernel,
        grid=(slots,),
        in_specs=[
            pl.BlockSpec((1, rows_i, rows_j, blocks), lambda k: (k, 0, 0, 0)),
            pl.BlockSpec((blocks, width), lambda k: (0, 0)),
            pl.BlockSpec((blocks, width), lambda k: (0, 0)),
        ],
        out_specs=[
            pl.BlockSpec((1, rows_i, rows_j, width), lambda k: (k, 0, 0, 0)),
            pl.BlockSpec((1, rows_i, rows_j, width), lambda k: (k, 0, 0, 0)),
        ],
        out_shape=[out, out],
    )(stiffness, pick_lo, pick_hi)


def merge_kernel(s_ref, lo_ref, hi_ref, place_lo_ref, place_hi_ref, arrival_ref, out_ref):
    rows, depth, blocks = s_ref.shape[1:]
    width = lo_ref.shape[-1]
    placed = jnp.dot(
        lo_ref[0].reshape(rows * depth, width), place_lo_ref[...],
        preferred_element_type=jnp.float32,
    ) + jnp.dot(
        hi_ref[0].reshape(rows * depth, width), place_hi_ref[...],
        preferred_element_type=jnp.float32,
    )
    placed = placed.reshape(rows, depth, blocks).astype(out_ref.dtype)
    out_ref[0] = jnp.where(arrival_ref[...] > 0, placed, s_ref[0])


def merge_arrived(stiffness, arrived_lo, arrived_hi, place_lo, place_hi, arrival):
    slots, rows_i, rows_j, blocks = stiffness.shape
    width = arrived_lo.shape[-1]
    return pl.pallas_call(
        merge_kernel,
        grid=(slots,),
        in_specs=[
            pl.BlockSpec((1, rows_i, rows_j, blocks), lambda k: (k, 0, 0, 0)),
            pl.BlockSpec((1, rows_i, rows_j, width), lambda k: (k, 0, 0, 0)),
            pl.BlockSpec((1, rows_i, rows_j, width), lambda k: (k, 0, 0, 0)),
            pl.BlockSpec((width, blocks), lambda k: (0, 0)),
            pl.BlockSpec((width, blocks), lambda k: (0, 0)),
            pl.BlockSpec((1, blocks), lambda k: (0, 0)),
        ],
        out_specs=pl.BlockSpec((1, rows_i, rows_j, blocks), lambda k: (k, 0, 0, 0)),
        out_shape=jax.ShapeDtypeStruct(stiffness.shape, stiffness.dtype),
    )(stiffness, arrived_lo, arrived_hi, place_lo, place_hi, arrival)


def force_kernel(s_ref, n_ref, out_ref):
    slots, rows = s_ref.shape[:2]
    for row in range(rows):
        acc = s_ref[0, row].astype(jnp.float32) * n_ref[0]
        for slot_index in range(1, slots):
            acc = acc + s_ref[slot_index, row].astype(jnp.float32) * n_ref[slot_index]
        out_ref[pl.ds(row, 1), :] = jnp.sum(acc, axis=0, keepdims=True)


def block_force(stiffness, neighbours):
    slots, rows_i, rows_j, blocks = stiffness.shape
    return pl.pallas_call(
        force_kernel,
        grid=(rows_i // ROWS,),
        in_specs=[
            pl.BlockSpec((slots, ROWS, rows_j, blocks), lambda i: (0, i, 0, 0)),
            pl.BlockSpec((slots, rows_j, blocks), lambda i: (0, 0, 0)),
        ],
        out_specs=pl.BlockSpec((ROWS, blocks), lambda i: (i, 0)),
        out_shape=jax.ShapeDtypeStruct((rows_i, blocks), jnp.float32),
        cost_estimate=pl.CostEstimate(
            flops=2 * slots * rows_i * rows_j * blocks,
            bytes_accessed=stiffness.size * 2 + neighbours.size * 4 + rows_i * blocks * 4,
            transcendentals=0,
        ),
    )(stiffness, neighbours)


def on_device(
    displacement,
    velocity,
    external,
    mass_inverse,
    pattern,
    coupled,
    stiffness_old,
    history_old,
    decay_old,
    strain_map,
    send_slot,
    arrive_place,
    arrive_count,
):
    blocks = displacement.shape[-1]
    capacity = send_slot.shape[2]
    slots = stiffness_old.shape[0]
    lanes = jnp.arange(blocks, dtype=jnp.int32)

    leave_lo = (lanes[:, None] == send_slot[0, 0][None, :]).astype(jnp.bfloat16)
    leave_hi = (lanes[:, None] == send_slot[0, 1][None, :]).astype(jnp.bfloat16)
    stiff_to_lower, stiff_to_higher = gather_leaving(stiffness_old, leave_lo, leave_hi)
    stiff_lower, stiff_higher = neighbour_exchange("shaft", stiff_to_lower, stiff_to_higher)

    count_live = jnp.arange(capacity, dtype=jnp.int32)[None, :] < arrive_count[0][:, None]
    place_lo = (arrive_place[0, 0][:, None] == lanes[None, :]) & count_live[0][:, None]
    place_hi = (arrive_place[0, 1][:, None] == lanes[None, :]) & count_live[1][:, None]
    arrival = (jnp.any(place_lo, 0) | jnp.any(place_hi, 0)).astype(jnp.int32)[None, :]
    stiffness = merge_arrived(
        stiffness_old,
        stiff_lower,
        stiff_higher,
        place_lo.astype(jnp.bfloat16),
        place_hi.astype(jnp.bfloat16),
        arrival,
    )

    outgoing = send_slot[0].reshape(-1)
    filled = count_live.reshape(-1)
    target = jnp.where(filled, arrive_place[0].reshape(-1), blocks)
    placing = (
        jnp.arange(blocks + 1, dtype=jnp.int32)
        .at[target]
        .set(blocks + jnp.arange(2 * capacity, dtype=jnp.int32))[:blocks]
    )
    moving_state = jnp.concatenate(
        [jnp.take(history_old, outgoing, axis=1), jnp.take(decay_old, outgoing, axis=1)], 0
    )
    state_lower, state_higher = neighbour_exchange(
        "shaft", moving_state[:, :capacity], moving_state[:, capacity:]
    )
    state_arrived = jnp.concatenate([state_lower, state_higher], 1)
    depth = history_old.shape[0]
    history = jnp.take(jnp.concatenate([history_old, state_arrived[:depth]], 1), placing, axis=1)
    decay = jnp.take(jnp.concatenate([decay_old, state_arrived[depth:]], 1), placing, axis=1)

    moved = displacement[:, 0, :]
    speeds = velocity[:, 0, :]
    forcing = external[:, 0, :]
    scaling = mass_inverse[:, 0, :]
    live = jnp.arange(slots, dtype=jnp.int32)[:, None] < coupled[0][None, :]
    codes = jnp.where(live, pattern[:, 0, :], 9)[:, None, :]
    for repeat in range(ITERS):
        rounded = moved.astype(jnp.bfloat16)[:, None, :]
        padded = padded_2(rounded, (("shaft", 2), ("ply", 1)), 1)
        neighbours = jnp.zeros((slots,) + moved.shape, jnp.bfloat16)
        for code_index in range(9):
            shifted = padded[:, code_index // 3, code_index % 3 : code_index % 3 + blocks]
            neighbours = jnp.where(codes == code_index, shifted[None], neighbours)
        product = stiffness.astype(jnp.float32) * neighbours.astype(jnp.float32)[:, None, :, :]
        force = jnp.sum(product, axis=(0, 2)) + jnp.dot(
            strain_map.T, history, precision=lax.Precision.HIGHEST
        )
        speeds = speeds + time_step * (scaling * (forcing - force))
        advanced = moved + time_step * speeds
        history = decay * history + jnp.dot(
            strain_map, advanced - moved, precision=lax.Precision.HIGHEST
        )
        moved = advanced
    return (moved[:, None, :], speeds[:, None, :], history[:, None, :])


def solution(mesh):
    in_specs = (
        P(None, "ply", "shaft"),
        P(None, "ply", "shaft"),
        P(None, "ply", "shaft"),
        P(None, "ply", "shaft"),
        P(None, "ply", "shaft"),
        P("ply", "shaft"),
        P(None, None, None, ("shaft", "ply")),
        P(None, ("shaft", "ply")),
        P(None, ("shaft", "ply")),
        P(),
        P(("shaft", "ply"), None, None),
        P(("shaft", "ply"), None, None),
        P(("shaft", "ply"), None),
    )
    out_specs = (P(None, "ply", "shaft"), P(None, "ply", "shaft"), P(None, "ply", "shaft"))
    return jax.shard_map(
        on_device, mesh=mesh, in_specs=in_specs, out_specs=out_specs, check_vma=False
    )
```

```python
import jax
import jax.numpy as jnp
from jax import lax
from jax.experimental import pallas as pl
from jax.experimental.pallas import tpu as pltpu
from jax.sharding import PartitionSpec as P

ITERS = 4
ROWS = 8


time_step = 0.25


def padded_2(value, sides, width):
    for axis, dim in sides:
        size, length = (lax.axis_size(axis), value.shape[dim])
        up = [(i, (i + 1) % size) for i in range(size - 1)]
        down = [(j, i) for i, j in up]
        last = lax.slice_in_dim(value, length - width, length, axis=dim)
        first = lax.slice_in_dim(value, 0, width, axis=dim)
        before = lax.ppermute(last, axis, up)
        after = lax.ppermute(first, axis, down)
        value = jnp.concatenate([before, value, after], axis=dim)
    return value


def neighbour_exchange(axis, lower_bound, upper_bound):
    size = lax.axis_size(axis)
    up = [(i, i + 1) for i in range(size - 1)]
    down = [(i + 1, i) for i in range(size - 1)]
    from_lower = lax.ppermute(upper_bound, axis, up)
    from_higher = lax.ppermute(lower_bound, axis, down)
    return from_lower, from_higher


def gather_kernel(s_ref, lo_ref, hi_ref, out_lo_ref, out_hi_ref):
    flat = s_ref[0]
    for pick_ref, out_ref in ((lo_ref, out_lo_ref), (hi_ref, out_hi_ref)):
        picked = lax.dot_general(
            pick_ref[...], flat, (((1,), (1,)), ((), ())), preferred_element_type=jnp.float32
        )
        out_ref[0] = picked.astype(out_ref.dtype)


def gather_leaving(stiffness, pick_lo, pick_hi):
    slots, depth, blocks = stiffness.shape
    width = pick_lo.shape[0]
    out = jax.ShapeDtypeStruct((slots, width, depth), stiffness.dtype)
    return pl.pallas_call(
        gather_kernel,
        grid=(slots,),
        in_specs=[
            pl.BlockSpec((1, depth, blocks), lambda k: (k, 0, 0)),
            pl.BlockSpec((width, blocks), lambda k: (0, 0)),
            pl.BlockSpec((width, blocks), lambda k: (0, 0)),
        ],
        out_specs=[
            pl.BlockSpec((1, width, depth), lambda k: (k, 0, 0)),
            pl.BlockSpec((1, width, depth), lambda k: (k, 0, 0)),
        ],
        out_shape=[out, out],
    )(stiffness, pick_lo, pick_hi)


def merge_kernel(s_ref, lo_ref, hi_ref, place_lo_ref, place_hi_ref, arrival_ref, out_ref):
    placed = jnp.dot(
        lo_ref[0].T, place_lo_ref[...], preferred_element_type=jnp.float32
    ) + jnp.dot(hi_ref[0].T, place_hi_ref[...], preferred_element_type=jnp.float32)
    out_ref[0] = jnp.where(arrival_ref[...] > 0, placed.astype(out_ref.dtype), s_ref[0])


def merge_arrived(stiffness, arrived_lo, arrived_hi, place_lo, place_hi, arrival):
    slots, depth, blocks = stiffness.shape
    width = arrived_lo.shape[1]
    return pl.pallas_call(
        merge_kernel,
        grid=(slots,),
        in_specs=[
            pl.BlockSpec((1, depth, blocks), lambda k: (k, 0, 0)),
            pl.BlockSpec((1, width, depth), lambda k: (k, 0, 0)),
            pl.BlockSpec((1, width, depth), lambda k: (k, 0, 0)),
            pl.BlockSpec((width, blocks), lambda k: (0, 0)),
            pl.BlockSpec((width, blocks), lambda k: (0, 0)),
            pl.BlockSpec((1, blocks), lambda k: (0, 0)),
        ],
        out_specs=pl.BlockSpec((1, depth, blocks), lambda k: (k, 0, 0)),
        out_shape=jax.ShapeDtypeStruct(stiffness.shape, stiffness.dtype),
    )(stiffness, arrived_lo, arrived_hi, place_lo, place_hi, arrival)


def force_kernel(s_ref, n_ref, out_ref):
    slots, rows = s_ref.shape[:2]
    for row in range(rows):
        acc = s_ref[0, row].astype(jnp.float32) * n_ref[0]
        for slot_index in range(1, slots):
            acc = acc + s_ref[slot_index, row].astype(jnp.float32) * n_ref[slot_index]
        out_ref[pl.ds(row, 1), :] = jnp.sum(acc, axis=0, keepdims=True)


def block_force(stiffness, neighbours):
    slots, rows_i, rows_j, blocks = stiffness.shape
    return pl.pallas_call(
        force_kernel,
        grid=(rows_i // ROWS,),
        in_specs=[
            pl.BlockSpec((slots, ROWS, rows_j, blocks), lambda i: (0, i, 0, 0)),
            pl.BlockSpec((slots, rows_j, blocks), lambda i: (0, 0, 0)),
        ],
        out_specs=pl.BlockSpec((ROWS, blocks), lambda i: (i, 0)),
        out_shape=jax.ShapeDtypeStruct((rows_i, blocks), jnp.float32),
        cost_estimate=pl.CostEstimate(
            flops=2 * slots * rows_i * rows_j * blocks,
            bytes_accessed=stiffness.size * 2 + neighbours.size * 4 + rows_i * blocks * 4,
            transcendentals=0,
        ),
    )(stiffness, neighbours)


def on_device(
    displacement,
    velocity,
    external,
    mass_inverse,
    pattern,
    coupled,
    stiffness_old,
    history_old,
    decay_old,
    strain_map,
    send_slot,
    arrive_place,
    arrive_count,
):
    blocks = displacement.shape[-1]
    capacity = send_slot.shape[2]
    slots = stiffness_old.shape[0]
    lanes = jnp.arange(blocks, dtype=jnp.int32)

    slots, rows_i, rows_j, _ = stiffness_old.shape
    stiff_flat = stiffness_old.reshape(slots, rows_i * rows_j, blocks)
    leave_lo = (send_slot[0, 0][:, None] == lanes[None, :]).astype(jnp.bfloat16)
    leave_hi = (send_slot[0, 1][:, None] == lanes[None, :]).astype(jnp.bfloat16)
    stiff_to_lower, stiff_to_higher = gather_leaving(stiff_flat, leave_lo, leave_hi)
    stiff_lower, stiff_higher = neighbour_exchange("shaft", stiff_to_lower, stiff_to_higher)

    count_live = jnp.arange(capacity, dtype=jnp.int32)[None, :] < arrive_count[0][:, None]
    place_lo = (arrive_place[0, 0][:, None] == lanes[None, :]) & count_live[0][:, None]
    place_hi = (arrive_place[0, 1][:, None] == lanes[None, :]) & count_live[1][:, None]
    arrival = (jnp.any(place_lo, 0) | jnp.any(place_hi, 0)).astype(jnp.int32)[None, :]
    stiffness = merge_arrived(
        stiff_flat,
        stiff_lower,
        stiff_higher,
        place_lo.astype(jnp.bfloat16),
        place_hi.astype(jnp.bfloat16),
        arrival,
    ).reshape(stiffness_old.shape)

    outgoing = send_slot[0].reshape(-1)
    filled = count_live.reshape(-1)
    target = jnp.where(filled, arrive_place[0].reshape(-1), blocks)
    placing = (
        jnp.arange(blocks + 1, dtype=jnp.int32)
        .at[target]
        .set(blocks + jnp.arange(2 * capacity, dtype=jnp.int32))[:blocks]
    )
    moving_state = jnp.concatenate(
        [jnp.take(history_old, outgoing, axis=1), jnp.take(decay_old, outgoing, axis=1)], 0
    )
    state_lower, state_higher = neighbour_exchange(
        "shaft", moving_state[:, :capacity], moving_state[:, capacity:]
    )
    state_arrived = jnp.concatenate([state_lower, state_higher], 1)
    depth = history_old.shape[0]
    history = jnp.take(jnp.concatenate([history_old, state_arrived[:depth]], 1), placing, axis=1)
    decay = jnp.take(jnp.concatenate([decay_old, state_arrived[depth:]], 1), placing, axis=1)

    moved = displacement[:, 0, :]
    speeds = velocity[:, 0, :]
    forcing = external[:, 0, :]
    scaling = mass_inverse[:, 0, :]
    live = jnp.arange(slots, dtype=jnp.int32)[:, None] < coupled[0][None, :]
    codes = jnp.where(live, pattern[:, 0, :], 9)[:, None, :]
    for repeat in range(ITERS):
        rounded = moved.astype(jnp.bfloat16)[:, None, :]
        padded = padded_2(rounded, (("shaft", 2), ("ply", 1)), 1)
        neighbours = jnp.zeros((slots,) + moved.shape, jnp.bfloat16)
        for code_index in range(9):
            shifted = padded[:, code_index // 3, code_index % 3 : code_index % 3 + blocks]
            neighbours = jnp.where(codes == code_index, shifted[None], neighbours)
        product = stiffness.astype(jnp.float32) * neighbours.astype(jnp.float32)[:, None, :, :]
        force = jnp.sum(product, axis=(0, 2)) + jnp.dot(
            strain_map.T, history, precision=lax.Precision.HIGHEST
        )
        speeds = speeds + time_step * (scaling * (forcing - force))
        advanced = moved + time_step * speeds
        history = decay * history + jnp.dot(
            strain_map, advanced - moved, precision=lax.Precision.HIGHEST
        )
        moved = advanced
    return (moved[:, None, :], speeds[:, None, :], history[:, None, :])


def solution(mesh):
    in_specs = (
        P(None, "ply", "shaft"),
        P(None, "ply", "shaft"),
        P(None, "ply", "shaft"),
        P(None, "ply", "shaft"),
        P(None, "ply", "shaft"),
        P("ply", "shaft"),
        P(None, None, None, ("shaft", "ply")),
        P(None, ("shaft", "ply")),
        P(None, ("shaft", "ply")),
        P(),
        P(("shaft", "ply"), None, None),
        P(("shaft", "ply"), None, None),
        P(("shaft", "ply"), None),
    )
    out_specs = (P(None, "ply", "shaft"), P(None, "ply", "shaft"), P(None, "ply", "shaft"))
    return jax.shard_map(
        on_device, mesh=mesh, in_specs=in_specs, out_specs=out_specs, check_vma=False
    )
```

```python
import jax
import jax.numpy as jnp
from jax import lax
from jax.experimental import pallas as pl
from jax.experimental.pallas import tpu as pltpu
from jax.sharding import PartitionSpec as P

ITERS = 4
ROWS = 8


time_step = 0.25


def padded_2(value, sides, width):
    for axis, dim in sides:
        size, length = (lax.axis_size(axis), value.shape[dim])
        up = [(i, (i + 1) % size) for i in range(size - 1)]
        down = [(j, i) for i, j in up]
        last = lax.slice_in_dim(value, length - width, length, axis=dim)
        first = lax.slice_in_dim(value, 0, width, axis=dim)
        before = lax.ppermute(last, axis, up)
        after = lax.ppermute(first, axis, down)
        value = jnp.concatenate([before, value, after], axis=dim)
    return value


def neighbour_exchange(axis, lower_bound, upper_bound):
    size = lax.axis_size(axis)
    up = [(i, i + 1) for i in range(size - 1)]
    down = [(i + 1, i) for i in range(size - 1)]
    from_lower = lax.ppermute(upper_bound, axis, up)
    from_higher = lax.ppermute(lower_bound, axis, down)
    return from_lower, from_higher


def gather_kernel(s_ref, lo_ref, hi_ref, out_lo_ref, out_hi_ref):
    flat = s_ref[0]
    for pick_ref, out_ref in ((lo_ref, out_lo_ref), (hi_ref, out_hi_ref)):
        picked = lax.dot_general(
            pick_ref[...], flat, (((1,), (1,)), ((), ())), preferred_element_type=jnp.float32
        )
        out_ref[0] = picked.astype(out_ref.dtype)


def gather_leaving(stiffness, pick_lo, pick_hi):
    slots, depth, blocks = stiffness.shape
    width = pick_lo.shape[0]
    out = jax.ShapeDtypeStruct((slots, width, depth), stiffness.dtype)
    return pl.pallas_call(
        gather_kernel,
        grid=(slots,),
        in_specs=[
            pl.BlockSpec((1, depth, blocks), lambda k: (k, 0, 0)),
            pl.BlockSpec((width, blocks), lambda k: (0, 0)),
            pl.BlockSpec((width, blocks), lambda k: (0, 0)),
        ],
        out_specs=[
            pl.BlockSpec((1, width, depth), lambda k: (k, 0, 0)),
            pl.BlockSpec((1, width, depth), lambda k: (k, 0, 0)),
        ],
        out_shape=[out, out],
    )(stiffness, pick_lo, pick_hi)


def merge_kernel(s_ref, lo_ref, hi_ref, place_lo_ref, place_hi_ref, arrival_ref, out_ref):
    placed = jnp.dot(
        lo_ref[0].T, place_lo_ref[...], preferred_element_type=jnp.float32
    ) + jnp.dot(hi_ref[0].T, place_hi_ref[...], preferred_element_type=jnp.float32)
    placed = placed.astype(out_ref.dtype).reshape(s_ref.shape[1:])
    out_ref[0] = jnp.where(arrival_ref[...] > 0, placed, s_ref[0])


def merge_arrived(stiffness, arrived_lo, arrived_hi, place_lo, place_hi, arrival):
    slots, rows_i, rows_j, blocks = stiffness.shape
    depth = rows_i * rows_j
    width = arrived_lo.shape[1]
    return pl.pallas_call(
        merge_kernel,
        grid=(slots,),
        in_specs=[
            pl.BlockSpec((1, rows_i, rows_j, blocks), lambda k: (k, 0, 0, 0)),
            pl.BlockSpec((1, width, depth), lambda k: (k, 0, 0)),
            pl.BlockSpec((1, width, depth), lambda k: (k, 0, 0)),
            pl.BlockSpec((width, blocks), lambda k: (0, 0)),
            pl.BlockSpec((width, blocks), lambda k: (0, 0)),
            pl.BlockSpec((1, blocks), lambda k: (0, 0)),
        ],
        out_specs=pl.BlockSpec((1, rows_i, rows_j, blocks), lambda k: (k, 0, 0, 0)),
        out_shape=jax.ShapeDtypeStruct(stiffness.shape, stiffness.dtype),
    )(stiffness, arrived_lo, arrived_hi, place_lo, place_hi, arrival)


def force_kernel(s_ref, n_ref, out_ref):
    slots, rows = s_ref.shape[:2]
    for row in range(rows):
        acc = s_ref[0, row].astype(jnp.float32) * n_ref[0]
        for slot_index in range(1, slots):
            acc = acc + s_ref[slot_index, row].astype(jnp.float32) * n_ref[slot_index]
        out_ref[pl.ds(row, 1), :] = jnp.sum(acc, axis=0, keepdims=True)


def block_force(stiffness, neighbours):
    slots, rows_i, rows_j, blocks = stiffness.shape
    return pl.pallas_call(
        force_kernel,
        grid=(rows_i // ROWS,),
        in_specs=[
            pl.BlockSpec((slots, ROWS, rows_j, blocks), lambda i: (0, i, 0, 0)),
            pl.BlockSpec((slots, rows_j, blocks), lambda i: (0, 0, 0)),
        ],
        out_specs=pl.BlockSpec((ROWS, blocks), lambda i: (i, 0)),
        out_shape=jax.ShapeDtypeStruct((rows_i, blocks), jnp.float32),
        cost_estimate=pl.CostEstimate(
            flops=2 * slots * rows_i * rows_j * blocks,
            bytes_accessed=stiffness.size * 2 + neighbours.size * 4 + rows_i * blocks * 4,
            transcendentals=0,
        ),
    )(stiffness, neighbours)


def on_device(
    displacement,
    velocity,
    external,
    mass_inverse,
    pattern,
    coupled,
    stiffness_old,
    history_old,
    decay_old,
    strain_map,
    send_slot,
    arrive_place,
    arrive_count,
):
    blocks = displacement.shape[-1]
    capacity = send_slot.shape[2]
    slots = stiffness_old.shape[0]
    lanes = jnp.arange(blocks, dtype=jnp.int32)

    slots, rows_i, rows_j, _ = stiffness_old.shape
    stiff_flat = stiffness_old.reshape(slots, rows_i * rows_j, blocks)
    leave_lo = (send_slot[0, 0][:, None] == lanes[None, :]).astype(jnp.bfloat16)
    leave_hi = (send_slot[0, 1][:, None] == lanes[None, :]).astype(jnp.bfloat16)
    stiff_to_lower, stiff_to_higher = gather_leaving(stiff_flat, leave_lo, leave_hi)
    stiff_lower, stiff_higher = neighbour_exchange("shaft", stiff_to_lower, stiff_to_higher)

    count_live = jnp.arange(capacity, dtype=jnp.int32)[None, :] < arrive_count[0][:, None]
    place_lo = (arrive_place[0, 0][:, None] == lanes[None, :]) & count_live[0][:, None]
    place_hi = (arrive_place[0, 1][:, None] == lanes[None, :]) & count_live[1][:, None]
    arrival = (jnp.any(place_lo, 0) | jnp.any(place_hi, 0)).astype(jnp.int32)[None, :]
    stiffness = merge_arrived(
        stiffness_old,
        stiff_lower,
        stiff_higher,
        place_lo.astype(jnp.bfloat16),
        place_hi.astype(jnp.bfloat16),
        arrival,
    )

    outgoing = send_slot[0].reshape(-1)
    filled = count_live.reshape(-1)
    target = jnp.where(filled, arrive_place[0].reshape(-1), blocks)
    placing = (
        jnp.arange(blocks + 1, dtype=jnp.int32)
        .at[target]
        .set(blocks + jnp.arange(2 * capacity, dtype=jnp.int32))[:blocks]
    )
    moving_state = jnp.concatenate(
        [jnp.take(history_old, outgoing, axis=1), jnp.take(decay_old, outgoing, axis=1)], 0
    )
    state_lower, state_higher = neighbour_exchange(
        "shaft", moving_state[:, :capacity], moving_state[:, capacity:]
    )
    state_arrived = jnp.concatenate([state_lower, state_higher], 1)
    depth = history_old.shape[0]
    history = jnp.take(jnp.concatenate([history_old, state_arrived[:depth]], 1), placing, axis=1)
    decay = jnp.take(jnp.concatenate([decay_old, state_arrived[depth:]], 1), placing, axis=1)

    moved = displacement[:, 0, :]
    speeds = velocity[:, 0, :]
    forcing = external[:, 0, :]
    scaling = mass_inverse[:, 0, :]
    live = jnp.arange(slots, dtype=jnp.int32)[:, None] < coupled[0][None, :]
    codes = jnp.where(live, pattern[:, 0, :], 9)[:, None, :]
    for repeat in range(ITERS):
        rounded = moved.astype(jnp.bfloat16)[:, None, :]
        padded = padded_2(rounded, (("shaft", 2), ("ply", 1)), 1)
        neighbours = jnp.zeros((slots,) + moved.shape, jnp.bfloat16)
        for code_index in range(9):
            shifted = padded[:, code_index // 3, code_index % 3 : code_index % 3 + blocks]
            neighbours = jnp.where(codes == code_index, shifted[None], neighbours)
        product = stiffness.astype(jnp.float32) * neighbours.astype(jnp.float32)[:, None, :, :]
        force = jnp.sum(product, axis=(0, 2)) + jnp.dot(
            strain_map.T, history, precision=lax.Precision.HIGHEST
        )
        speeds = speeds + time_step * (scaling * (forcing - force))
        advanced = moved + time_step * speeds
        history = decay * history + jnp.dot(
            strain_map, advanced - moved, precision=lax.Precision.HIGHEST
        )
        moved = advanced
    return (moved[:, None, :], speeds[:, None, :], history[:, None, :])


def solution(mesh):
    in_specs = (
        P(None, "ply", "shaft"),
        P(None, "ply", "shaft"),
        P(None, "ply", "shaft"),
        P(None, "ply", "shaft"),
        P(None, "ply", "shaft"),
        P("ply", "shaft"),
        P(None, None, None, ("shaft", "ply")),
        P(None, ("shaft", "ply")),
        P(None, ("shaft", "ply")),
        P(),
        P(("shaft", "ply"), None, None),
        P(("shaft", "ply"), None, None),
        P(("shaft", "ply"), None),
    )
    out_specs = (P(None, "ply", "shaft"), P(None, "ply", "shaft"), P(None, "ply", "shaft"))
    return jax.shard_map(
        on_device, mesh=mesh, in_specs=in_specs, out_specs=out_specs, check_vma=False
    )
```

```python
import jax
import jax.numpy as jnp
from jax import lax
from jax.experimental import pallas as pl
from jax.experimental.pallas import tpu as pltpu
from jax.sharding import PartitionSpec as P

ITERS = 4
ROWS = 8


time_step = 0.25


def padded_2(value, sides, width):
    for axis, dim in sides:
        size, length = (lax.axis_size(axis), value.shape[dim])
        up = [(i, (i + 1) % size) for i in range(size - 1)]
        down = [(j, i) for i, j in up]
        last = lax.slice_in_dim(value, length - width, length, axis=dim)
        first = lax.slice_in_dim(value, 0, width, axis=dim)
        before = lax.ppermute(last, axis, up)
        after = lax.ppermute(first, axis, down)
        value = jnp.concatenate([before, value, after], axis=dim)
    return value


def ply_rows(row):
    size = lax.axis_size("ply")
    here = lax.axis_index("ply")
    gathered = lax.all_gather(row, "ply")
    lower = lax.dynamic_index_in_dim(gathered, jnp.maximum(here - 1, 0), 0, keepdims=False)
    upper = lax.dynamic_index_in_dim(gathered, jnp.minimum(here + 1, size - 1), 0, keepdims=False)
    lower = jnp.where(here > 0, lower, jnp.zeros_like(lower))
    upper = jnp.where(here < size - 1, upper, jnp.zeros_like(upper))
    return jnp.stack([lower, row, upper], 1)


def neighbour_exchange(axis, lower_bound, upper_bound):
    size = lax.axis_size(axis)
    up = [(i, i + 1) for i in range(size - 1)]
    down = [(i + 1, i) for i in range(size - 1)]
    from_lower = lax.ppermute(upper_bound, axis, up)
    from_higher = lax.ppermute(lower_bound, axis, down)
    return from_lower, from_higher


def gather_kernel(s_ref, lo_ref, hi_ref, out_lo_ref, out_hi_ref):
    flat = s_ref[0]
    for pick_ref, out_ref in ((lo_ref, out_lo_ref), (hi_ref, out_hi_ref)):
        picked = lax.dot_general(
            pick_ref[...], flat, (((1,), (1,)), ((), ())), preferred_element_type=jnp.float32
        )
        out_ref[0] = picked.astype(out_ref.dtype)


def gather_leaving(stiffness, pick_lo, pick_hi):
    slots, depth, blocks = stiffness.shape
    width = pick_lo.shape[0]
    out = jax.ShapeDtypeStruct((slots, width, depth), stiffness.dtype)
    return pl.pallas_call(
        gather_kernel,
        grid=(slots,),
        in_specs=[
            pl.BlockSpec((1, depth, blocks), lambda k: (k, 0, 0)),
            pl.BlockSpec((width, blocks), lambda k: (0, 0)),
            pl.BlockSpec((width, blocks), lambda k: (0, 0)),
        ],
        out_specs=[
            pl.BlockSpec((1, width, depth), lambda k: (k, 0, 0)),
            pl.BlockSpec((1, width, depth), lambda k: (k, 0, 0)),
        ],
        out_shape=[out, out],
    )(stiffness, pick_lo, pick_hi)


def merge_kernel(s_ref, lo_ref, hi_ref, place_lo_ref, place_hi_ref, arrival_ref, out_ref):
    placed = jnp.dot(
        lo_ref[0].T, place_lo_ref[...], preferred_element_type=jnp.float32
    ) + jnp.dot(hi_ref[0].T, place_hi_ref[...], preferred_element_type=jnp.float32)
    placed = placed.astype(out_ref.dtype).reshape(s_ref.shape[1:])
    out_ref[0] = jnp.where(arrival_ref[...] > 0, placed, s_ref[0])


def merge_arrived(stiffness, arrived_lo, arrived_hi, place_lo, place_hi, arrival):
    slots, rows_i, rows_j, blocks = stiffness.shape
    depth = rows_i * rows_j
    width = arrived_lo.shape[1]
    return pl.pallas_call(
        merge_kernel,
        grid=(slots,),
        in_specs=[
            pl.BlockSpec((1, rows_i, rows_j, blocks), lambda k: (k, 0, 0, 0)),
            pl.BlockSpec((1, width, depth), lambda k: (k, 0, 0)),
            pl.BlockSpec((1, width, depth), lambda k: (k, 0, 0)),
            pl.BlockSpec((width, blocks), lambda k: (0, 0)),
            pl.BlockSpec((width, blocks), lambda k: (0, 0)),
            pl.BlockSpec((1, blocks), lambda k: (0, 0)),
        ],
        out_specs=pl.BlockSpec((1, rows_i, rows_j, blocks), lambda k: (k, 0, 0, 0)),
        out_shape=jax.ShapeDtypeStruct(stiffness.shape, stiffness.dtype),
    )(stiffness, arrived_lo, arrived_hi, place_lo, place_hi, arrival)


def force_kernel(s_ref, n_ref, out_ref):
    slots, rows = s_ref.shape[:2]
    for row in range(rows):
        acc = s_ref[0, row].astype(jnp.float32) * n_ref[0]
        for slot_index in range(1, slots):
            acc = acc + s_ref[slot_index, row].astype(jnp.float32) * n_ref[slot_index]
        out_ref[pl.ds(row, 1), :] = jnp.sum(acc, axis=0, keepdims=True)


def block_force(stiffness, neighbours):
    slots, rows_i, rows_j, blocks = stiffness.shape
    return pl.pallas_call(
        force_kernel,
        grid=(rows_i // ROWS,),
        in_specs=[
            pl.BlockSpec((slots, ROWS, rows_j, blocks), lambda i: (0, i, 0, 0)),
            pl.BlockSpec((slots, rows_j, blocks), lambda i: (0, 0, 0)),
        ],
        out_specs=pl.BlockSpec((ROWS, blocks), lambda i: (i, 0)),
        out_shape=jax.ShapeDtypeStruct((rows_i, blocks), jnp.float32),
        cost_estimate=pl.CostEstimate(
            flops=2 * slots * rows_i * rows_j * blocks,
            bytes_accessed=stiffness.size * 2 + neighbours.size * 4 + rows_i * blocks * 4,
            transcendentals=0,
        ),
    )(stiffness, neighbours)


def on_device(
    displacement,
    velocity,
    external,
    mass_inverse,
    pattern,
    coupled,
    stiffness_old,
    history_old,
    decay_old,
    strain_map,
    send_slot,
    arrive_place,
    arrive_count,
):
    blocks = displacement.shape[-1]
    capacity = send_slot.shape[2]
    slots = stiffness_old.shape[0]
    lanes = jnp.arange(blocks, dtype=jnp.int32)

    slots, rows_i, rows_j, _ = stiffness_old.shape
    stiff_flat = stiffness_old.reshape(slots, rows_i * rows_j, blocks)
    leave_lo = (send_slot[0, 0][:, None] == lanes[None, :]).astype(jnp.bfloat16)
    leave_hi = (send_slot[0, 1][:, None] == lanes[None, :]).astype(jnp.bfloat16)
    stiff_to_lower, stiff_to_higher = gather_leaving(stiff_flat, leave_lo, leave_hi)
    stiff_lower, stiff_higher = neighbour_exchange("shaft", stiff_to_lower, stiff_to_higher)

    count_live = jnp.arange(capacity, dtype=jnp.int32)[None, :] < arrive_count[0][:, None]
    place_lo = (arrive_place[0, 0][:, None] == lanes[None, :]) & count_live[0][:, None]
    place_hi = (arrive_place[0, 1][:, None] == lanes[None, :]) & count_live[1][:, None]
    arrival = (jnp.any(place_lo, 0) | jnp.any(place_hi, 0)).astype(jnp.int32)[None, :]
    stiffness = merge_arrived(
        stiffness_old,
        stiff_lower,
        stiff_higher,
        place_lo.astype(jnp.bfloat16),
        place_hi.astype(jnp.bfloat16),
        arrival,
    )

    outgoing = send_slot[0].reshape(-1)
    filled = count_live.reshape(-1)
    target = jnp.where(filled, arrive_place[0].reshape(-1), blocks)
    placing = (
        jnp.arange(blocks + 1, dtype=jnp.int32)
        .at[target]
        .set(blocks + jnp.arange(2 * capacity, dtype=jnp.int32))[:blocks]
    )
    moving_state = jnp.concatenate(
        [jnp.take(history_old, outgoing, axis=1), jnp.take(decay_old, outgoing, axis=1)], 0
    )
    state_lower, state_higher = neighbour_exchange(
        "shaft", moving_state[:, :capacity], moving_state[:, capacity:]
    )
    state_arrived = jnp.concatenate([state_lower, state_higher], 1)
    depth = history_old.shape[0]
    history = jnp.take(jnp.concatenate([history_old, state_arrived[:depth]], 1), placing, axis=1)
    decay = jnp.take(jnp.concatenate([decay_old, state_arrived[depth:]], 1), placing, axis=1)

    moved = displacement[:, 0, :]
    speeds = velocity[:, 0, :]
    forcing = external[:, 0, :]
    scaling = mass_inverse[:, 0, :]
    live = jnp.arange(slots, dtype=jnp.int32)[:, None] < coupled[0][None, :]
    codes = jnp.where(live, pattern[:, 0, :], 9)[:, None, :]
    for repeat in range(ITERS):
        rounded = moved.astype(jnp.bfloat16)[:, None, :]
        padded = ply_rows(padded_2(rounded, (("shaft", 2),), 1)[:, 0, :])
        neighbours = jnp.zeros((slots,) + moved.shape, jnp.bfloat16)
        for code_index in range(9):
            shifted = padded[:, code_index // 3, code_index % 3 : code_index % 3 + blocks]
            neighbours = jnp.where(codes == code_index, shifted[None], neighbours)
        product = stiffness.astype(jnp.float32) * neighbours.astype(jnp.float32)[:, None, :, :]
        force = jnp.sum(product, axis=(0, 2)) + jnp.dot(
            strain_map.T, history, precision=lax.Precision.HIGHEST
        )
        speeds = speeds + time_step * (scaling * (forcing - force))
        advanced = moved + time_step * speeds
        history = decay * history + jnp.dot(
            strain_map, advanced - moved, precision=lax.Precision.HIGHEST
        )
        moved = advanced
    return (moved[:, None, :], speeds[:, None, :], history[:, None, :])


def solution(mesh):
    in_specs = (
        P(None, "ply", "shaft"),
        P(None, "ply", "shaft"),
        P(None, "ply", "shaft"),
        P(None, "ply", "shaft"),
        P(None, "ply", "shaft"),
        P("ply", "shaft"),
        P(None, None, None, ("shaft", "ply")),
        P(None, ("shaft", "ply")),
        P(None, ("shaft", "ply")),
        P(),
        P(("shaft", "ply"), None, None),
        P(("shaft", "ply"), None, None),
        P(("shaft", "ply"), None),
    )
    out_specs = (P(None, "ply", "shaft"), P(None, "ply", "shaft"), P(None, "ply", "shaft"))
    return jax.shard_map(
        on_device, mesh=mesh, in_specs=in_specs, out_specs=out_specs, check_vma=False
    )
```

```python
import jax
import jax.numpy as jnp
from jax import lax
from jax.experimental import pallas as pl
from jax.experimental.pallas import tpu as pltpu
from jax.sharding import PartitionSpec as P

ITERS = 4
ROWS = 8


time_step = 0.25


def padded_2(value, sides, width):
    for axis, dim in sides:
        size, length = (lax.axis_size(axis), value.shape[dim])
        up = [(i, (i + 1) % size) for i in range(size - 1)]
        down = [(j, i) for i, j in up]
        last = lax.slice_in_dim(value, length - width, length, axis=dim)
        first = lax.slice_in_dim(value, 0, width, axis=dim)
        before = lax.ppermute(last, axis, up)
        after = lax.ppermute(first, axis, down)
        value = jnp.concatenate([before, value, after], axis=dim)
    return value


def neighbour_exchange(axis, lower_bound, upper_bound):
    size = lax.axis_size(axis)
    up = [(i, i + 1) for i in range(size - 1)]
    down = [(i + 1, i) for i in range(size - 1)]
    from_lower = lax.ppermute(upper_bound, axis, up)
    from_higher = lax.ppermute(lower_bound, axis, down)
    return from_lower, from_higher


def gather_kernel(s_ref, pick_ref, out_lo_ref, out_hi_ref):
    width = out_lo_ref.shape[0]
    picked = jnp.dot(s_ref[0], pick_ref[...], preferred_element_type=jnp.float32).T
    out_lo_ref[...] = picked[:width].astype(out_lo_ref.dtype)
    out_hi_ref[...] = picked[width : 2 * width].astype(out_hi_ref.dtype)


def gather_leaving(stiffness, slot_index, pick, width):
    slots, depth, blocks = stiffness.shape
    out = jax.ShapeDtypeStruct((width, depth), stiffness.dtype)
    return pl.pallas_call(
        gather_kernel,
        grid=(1,),
        in_specs=[
            pl.BlockSpec((1, depth, blocks), lambda g: (slot_index, 0, 0)),
            pl.BlockSpec(pick.shape, lambda g: (0, 0)),
        ],
        out_specs=[
            pl.BlockSpec((width, depth), lambda g: (0, 0)),
            pl.BlockSpec((width, depth), lambda g: (0, 0)),
        ],
        out_shape=[out, out],
    )(stiffness, pick)


def merge_kernel(s_ref, lo_ref, hi_ref, place_lo_ref, place_hi_ref, arrival_ref, out_ref):
    placed = jnp.dot(
        lo_ref[...].T, place_lo_ref[...], preferred_element_type=jnp.float32
    ) + jnp.dot(hi_ref[...].T, place_hi_ref[...], preferred_element_type=jnp.float32)
    placed = placed.astype(out_ref.dtype).reshape(out_ref.shape)
    out_ref[...] = jnp.where(arrival_ref[...] > 0, placed, s_ref[0])


def merge_arrived(stiffness, slot_index, arrived_lo, arrived_hi, place_lo, place_hi, arrival):
    slots, rows_i, rows_j, blocks = stiffness.shape
    width, depth = arrived_lo.shape
    return pl.pallas_call(
        merge_kernel,
        grid=(1,),
        in_specs=[
            pl.BlockSpec((1, rows_i, rows_j, blocks), lambda g: (slot_index, 0, 0, 0)),
            pl.BlockSpec((width, depth), lambda g: (0, 0)),
            pl.BlockSpec((width, depth), lambda g: (0, 0)),
            pl.BlockSpec((width, blocks), lambda g: (0, 0)),
            pl.BlockSpec((width, blocks), lambda g: (0, 0)),
            pl.BlockSpec((1, blocks), lambda g: (0, 0)),
        ],
        out_specs=pl.BlockSpec((rows_i, rows_j, blocks), lambda g: (0, 0, 0)),
        out_shape=jax.ShapeDtypeStruct((rows_i, rows_j, blocks), stiffness.dtype),
    )(stiffness, arrived_lo, arrived_hi, place_lo, place_hi, arrival)


def force_kernel(s_ref, n_ref, out_ref):
    slots, rows = s_ref.shape[:2]
    for row in range(rows):
        acc = s_ref[0, row].astype(jnp.float32) * n_ref[0]
        for slot_index in range(1, slots):
            acc = acc + s_ref[slot_index, row].astype(jnp.float32) * n_ref[slot_index]
        out_ref[pl.ds(row, 1), :] = jnp.sum(acc, axis=0, keepdims=True)


def block_force(stiffness, neighbours):
    slots, rows_i, rows_j, blocks = stiffness.shape
    return pl.pallas_call(
        force_kernel,
        grid=(rows_i // ROWS,),
        in_specs=[
            pl.BlockSpec((slots, ROWS, rows_j, blocks), lambda i: (0, i, 0, 0)),
            pl.BlockSpec((slots, rows_j, blocks), lambda i: (0, 0, 0)),
        ],
        out_specs=pl.BlockSpec((ROWS, blocks), lambda i: (i, 0)),
        out_shape=jax.ShapeDtypeStruct((rows_i, blocks), jnp.float32),
        cost_estimate=pl.CostEstimate(
            flops=2 * slots * rows_i * rows_j * blocks,
            bytes_accessed=stiffness.size * 2 + neighbours.size * 4 + rows_i * blocks * 4,
            transcendentals=0,
        ),
    )(stiffness, neighbours)


def on_device(
    displacement,
    velocity,
    external,
    mass_inverse,
    pattern,
    coupled,
    stiffness_old,
    history_old,
    decay_old,
    strain_map,
    send_slot,
    arrive_place,
    arrive_count,
):
    blocks = displacement.shape[-1]
    capacity = send_slot.shape[2]
    slots = stiffness_old.shape[0]
    lanes = jnp.arange(blocks, dtype=jnp.int32)

    slots, rows_i, rows_j, _ = stiffness_old.shape
    stiff_flat = stiffness_old.reshape(slots, rows_i * rows_j, blocks)
    picks = jnp.arange(128, dtype=jnp.int32)
    leaving = jnp.concatenate([send_slot[0, 0], send_slot[0, 1]])
    pick = (
        (lanes[:, None] == jnp.pad(leaving, (0, 128 - 2 * capacity))[None, :])
        & (picks < 2 * capacity)[None, :]
    ).astype(jnp.bfloat16)

    count_live = jnp.arange(capacity, dtype=jnp.int32)[None, :] < arrive_count[0][:, None]
    place_lo = (arrive_place[0, 0][:, None] == lanes[None, :]) & count_live[0][:, None]
    place_hi = (arrive_place[0, 1][:, None] == lanes[None, :]) & count_live[1][:, None]
    arrival = (jnp.any(place_lo, 0) | jnp.any(place_hi, 0)).astype(jnp.int32)[None, :]
    stiffness = []
    for slot_index in range(slots):
        to_lower, to_higher = gather_leaving(stiff_flat, slot_index, pick, capacity)
        arrived_lo, arrived_hi = neighbour_exchange("shaft", to_lower, to_higher)
        stiffness.append(
            merge_arrived(
                stiffness_old,
                slot_index,
                arrived_lo,
                arrived_hi,
                place_lo.astype(jnp.bfloat16),
                place_hi.astype(jnp.bfloat16),
                arrival,
            )
        )

    outgoing = send_slot[0].reshape(-1)
    filled = count_live.reshape(-1)
    target = jnp.where(filled, arrive_place[0].reshape(-1), blocks)
    placing = (
        jnp.arange(blocks + 1, dtype=jnp.int32)
        .at[target]
        .set(blocks + jnp.arange(2 * capacity, dtype=jnp.int32))[:blocks]
    )
    moving_state = jnp.concatenate(
        [jnp.take(history_old, outgoing, axis=1), jnp.take(decay_old, outgoing, axis=1)], 0
    )
    state_lower, state_higher = neighbour_exchange(
        "shaft", moving_state[:, :capacity], moving_state[:, capacity:]
    )
    state_arrived = jnp.concatenate([state_lower, state_higher], 1)
    depth = history_old.shape[0]
    history = jnp.take(jnp.concatenate([history_old, state_arrived[:depth]], 1), placing, axis=1)
    decay = jnp.take(jnp.concatenate([decay_old, state_arrived[depth:]], 1), placing, axis=1)

    moved = displacement[:, 0, :]
    speeds = velocity[:, 0, :]
    forcing = external[:, 0, :]
    scaling = mass_inverse[:, 0, :]
    live = jnp.arange(slots, dtype=jnp.int32)[:, None] < coupled[0][None, :]
    codes = jnp.where(live, pattern[:, 0, :], 9)[:, None, :]
    for repeat in range(ITERS):
        rounded = moved.astype(jnp.bfloat16)[:, None, :]
        padded = padded_2(rounded, (("shaft", 2), ("ply", 1)), 1)
        neighbours = jnp.zeros((slots,) + moved.shape, jnp.bfloat16)
        for code_index in range(9):
            shifted = padded[:, code_index // 3, code_index % 3 : code_index % 3 + blocks]
            neighbours = jnp.where(codes == code_index, shifted[None], neighbours)
        product = None
        for slot_index in range(slots):
            term = stiffness[slot_index].astype(jnp.float32) * neighbours[slot_index].astype(
                jnp.float32
            )[None, :, :]
            product = term if product is None else product + term
        force = jnp.sum(product, axis=1) + jnp.dot(
            strain_map.T, history, precision=lax.Precision.HIGHEST
        )
        speeds = speeds + time_step * (scaling * (forcing - force))
        advanced = moved + time_step * speeds
        history = decay * history + jnp.dot(
            strain_map, advanced - moved, precision=lax.Precision.HIGHEST
        )
        moved = advanced
    return (moved[:, None, :], speeds[:, None, :], history[:, None, :])


def solution(mesh):
    in_specs = (
        P(None, "ply", "shaft"),
        P(None, "ply", "shaft"),
        P(None, "ply", "shaft"),
        P(None, "ply", "shaft"),
        P(None, "ply", "shaft"),
        P("ply", "shaft"),
        P(None, None, None, ("shaft", "ply")),
        P(None, ("shaft", "ply")),
        P(None, ("shaft", "ply")),
        P(),
        P(("shaft", "ply"), None, None),
        P(("shaft", "ply"), None, None),
        P(("shaft", "ply"), None),
    )
    out_specs = (P(None, "ply", "shaft"), P(None, "ply", "shaft"), P(None, "ply", "shaft"))
    return jax.shard_map(
        on_device, mesh=mesh, in_specs=in_specs, out_specs=out_specs, check_vma=False
    )
```

```python
import jax
import jax.numpy as jnp
from jax import lax
from jax.experimental import pallas as pl
from jax.experimental.pallas import tpu as pltpu
from jax.sharding import PartitionSpec as P

ITERS = 4
ROWS = 8
SPLIT = 4


time_step = 0.25


def padded_2(value, sides, width):
    for axis, dim in sides:
        size, length = (lax.axis_size(axis), value.shape[dim])
        up = [(i, (i + 1) % size) for i in range(size - 1)]
        down = [(j, i) for i, j in up]
        last = lax.slice_in_dim(value, length - width, length, axis=dim)
        first = lax.slice_in_dim(value, 0, width, axis=dim)
        before = lax.ppermute(last, axis, up)
        after = lax.ppermute(first, axis, down)
        value = jnp.concatenate([before, value, after], axis=dim)
    return value


def neighbour_exchange(axis, lower_bound, upper_bound):
    size = lax.axis_size(axis)
    up = [(i, i + 1) for i in range(size - 1)]
    down = [(i + 1, i) for i in range(size - 1)]
    from_lower = lax.ppermute(upper_bound, axis, up)
    from_higher = lax.ppermute(lower_bound, axis, down)
    return from_lower, from_higher


def gather_kernel(s_ref, lo_ref, hi_ref, out_lo_ref, out_hi_ref):
    flat = s_ref[0]
    for pick_ref, out_ref in ((lo_ref, out_lo_ref), (hi_ref, out_hi_ref)):
        picked = lax.dot_general(
            pick_ref[...], flat, (((1,), (1,)), ((), ())), preferred_element_type=jnp.float32
        )
        out_ref[0] = picked.astype(out_ref.dtype)


def gather_leaving(stiffness, pick_lo, pick_hi):
    slots, depth, blocks = stiffness.shape
    width = pick_lo.shape[0]
    out = jax.ShapeDtypeStruct((slots, width, depth), stiffness.dtype)
    return pl.pallas_call(
        gather_kernel,
        grid=(slots, SPLIT),
        in_specs=[
            pl.BlockSpec((1, depth // SPLIT, blocks), lambda k, r: (k, r, 0)),
            pl.BlockSpec((width, blocks), lambda k, r: (0, 0)),
            pl.BlockSpec((width, blocks), lambda k, r: (0, 0)),
        ],
        out_specs=[
            pl.BlockSpec((1, width, depth // SPLIT), lambda k, r: (k, 0, r)),
            pl.BlockSpec((1, width, depth // SPLIT), lambda k, r: (k, 0, r)),
        ],
        out_shape=[out, out],
    )(stiffness, pick_lo, pick_hi)


def merge_kernel(s_ref, lo_ref, hi_ref, place_lo_ref, place_hi_ref, arrival_ref, out_ref):
    lhs_rows = (((0,), (0,)), ((), ()))
    placed = lax.dot_general(
        lo_ref[0], place_lo_ref[...], lhs_rows, preferred_element_type=jnp.float32
    ) + lax.dot_general(hi_ref[0], place_hi_ref[...], lhs_rows, preferred_element_type=jnp.float32)
    placed = placed.astype(out_ref.dtype).reshape(s_ref.shape[1:])
    out_ref[0] = jnp.where(arrival_ref[...] > 0, placed, s_ref[0])


def merge_arrived(stiffness, arrived_lo, arrived_hi, place_lo, place_hi, arrival):
    slots, rows_i, rows_j, blocks = stiffness.shape
    depth = rows_i * rows_j
    width = arrived_lo.shape[1]
    return pl.pallas_call(
        merge_kernel,
        grid=(slots, SPLIT),
        in_specs=[
            pl.BlockSpec((1, rows_i // SPLIT, rows_j, blocks), lambda k, r: (k, r, 0, 0)),
            pl.BlockSpec((1, width, depth // SPLIT), lambda k, r: (k, 0, r)),
            pl.BlockSpec((1, width, depth // SPLIT), lambda k, r: (k, 0, r)),
            pl.BlockSpec((width, blocks), lambda k, r: (0, 0)),
            pl.BlockSpec((width, blocks), lambda k, r: (0, 0)),
            pl.BlockSpec((1, blocks), lambda k, r: (0, 0)),
        ],
        out_specs=pl.BlockSpec((1, rows_i // SPLIT, rows_j, blocks), lambda k, r: (k, r, 0, 0)),
        out_shape=jax.ShapeDtypeStruct(stiffness.shape, stiffness.dtype),
    )(stiffness, arrived_lo, arrived_hi, place_lo, place_hi, arrival)


def force_kernel(s_ref, n_ref, out_ref):
    slots, rows = s_ref.shape[:2]
    for row in range(rows):
        acc = s_ref[0, row].astype(jnp.float32) * n_ref[0]
        for slot_index in range(1, slots):
            acc = acc + s_ref[slot_index, row].astype(jnp.float32) * n_ref[slot_index]
        out_ref[pl.ds(row, 1), :] = jnp.sum(acc, axis=0, keepdims=True)


def block_force(stiffness, neighbours):
    slots, rows_i, rows_j, blocks = stiffness.shape
    return pl.pallas_call(
        force_kernel,
        grid=(rows_i // ROWS,),
        in_specs=[
            pl.BlockSpec((slots, ROWS, rows_j, blocks), lambda i: (0, i, 0, 0)),
            pl.BlockSpec((slots, rows_j, blocks), lambda i: (0, 0, 0)),
        ],
        out_specs=pl.BlockSpec((ROWS, blocks), lambda i: (i, 0)),
        out_shape=jax.ShapeDtypeStruct((rows_i, blocks), jnp.float32),
        cost_estimate=pl.CostEstimate(
            flops=2 * slots * rows_i * rows_j * blocks,
            bytes_accessed=stiffness.size * 2 + neighbours.size * 4 + rows_i * blocks * 4,
            transcendentals=0,
        ),
    )(stiffness, neighbours)


def on_device(
    displacement,
    velocity,
    external,
    mass_inverse,
    pattern,
    coupled,
    stiffness_old,
    history_old,
    decay_old,
    strain_map,
    send_slot,
    arrive_place,
    arrive_count,
):
    blocks = displacement.shape[-1]
    capacity = send_slot.shape[2]
    slots = stiffness_old.shape[0]
    lanes = jnp.arange(blocks, dtype=jnp.int32)

    slots, rows_i, rows_j, _ = stiffness_old.shape
    stiff_flat = stiffness_old.reshape(slots, rows_i * rows_j, blocks)
    leave_lo = (send_slot[0, 0][:, None] == lanes[None, :]).astype(jnp.bfloat16)
    leave_hi = (send_slot[0, 1][:, None] == lanes[None, :]).astype(jnp.bfloat16)
    stiff_to_lower, stiff_to_higher = gather_leaving(stiff_flat, leave_lo, leave_hi)
    stiff_lower, stiff_higher = neighbour_exchange("shaft", stiff_to_lower, stiff_to_higher)

    count_live = jnp.arange(capacity, dtype=jnp.int32)[None, :] < arrive_count[0][:, None]
    place_lo = (arrive_place[0, 0][:, None] == lanes[None, :]) & count_live[0][:, None]
    place_hi = (arrive_place[0, 1][:, None] == lanes[None, :]) & count_live[1][:, None]
    arrival = (jnp.any(place_lo, 0) | jnp.any(place_hi, 0)).astype(jnp.int32)[None, :]
    stiffness = merge_arrived(
        stiffness_old,
        stiff_lower,
        stiff_higher,
        place_lo.astype(jnp.bfloat16),
        place_hi.astype(jnp.bfloat16),
        arrival,
    )

    outgoing = send_slot[0].reshape(-1)
    filled = count_live.reshape(-1)
    target = jnp.where(filled, arrive_place[0].reshape(-1), blocks)
    placing = (
        jnp.arange(blocks + 1, dtype=jnp.int32)
        .at[target]
        .set(blocks + jnp.arange(2 * capacity, dtype=jnp.int32))[:blocks]
    )
    moving_state = jnp.concatenate(
        [jnp.take(history_old, outgoing, axis=1), jnp.take(decay_old, outgoing, axis=1)], 0
    )
    state_lower, state_higher = neighbour_exchange(
        "shaft", moving_state[:, :capacity], moving_state[:, capacity:]
    )
    state_arrived = jnp.concatenate([state_lower, state_higher], 1)
    depth = history_old.shape[0]
    history = jnp.take(jnp.concatenate([history_old, state_arrived[:depth]], 1), placing, axis=1)
    decay = jnp.take(jnp.concatenate([decay_old, state_arrived[depth:]], 1), placing, axis=1)

    moved = displacement[:, 0, :]
    speeds = velocity[:, 0, :]
    forcing = external[:, 0, :]
    scaling = mass_inverse[:, 0, :]
    live = jnp.arange(slots, dtype=jnp.int32)[:, None] < coupled[0][None, :]
    codes = jnp.where(live, pattern[:, 0, :], 9)[:, None, :]
    for repeat in range(ITERS):
        rounded = moved.astype(jnp.bfloat16)[:, None, :]
        padded = padded_2(rounded, (("shaft", 2), ("ply", 1)), 1)
        neighbours = jnp.zeros((slots,) + moved.shape, jnp.bfloat16)
        for code_index in range(9):
            shifted = padded[:, code_index // 3, code_index % 3 : code_index % 3 + blocks]
            neighbours = jnp.where(codes == code_index, shifted[None], neighbours)
        product = stiffness.astype(jnp.float32) * neighbours.astype(jnp.float32)[:, None, :, :]
        force = jnp.sum(product, axis=(0, 2)) + jnp.dot(
            strain_map.T, history, precision=lax.Precision.HIGHEST
        )
        speeds = speeds + time_step * (scaling * (forcing - force))
        advanced = moved + time_step * speeds
        history = decay * history + jnp.dot(
            strain_map, advanced - moved, precision=lax.Precision.HIGHEST
        )
        moved = advanced
    return (moved[:, None, :], speeds[:, None, :], history[:, None, :])


def solution(mesh):
    in_specs = (
        P(None, "ply", "shaft"),
        P(None, "ply", "shaft"),
        P(None, "ply", "shaft"),
        P(None, "ply", "shaft"),
        P(None, "ply", "shaft"),
        P("ply", "shaft"),
        P(None, None, None, ("shaft", "ply")),
        P(None, ("shaft", "ply")),
        P(None, ("shaft", "ply")),
        P(),
        P(("shaft", "ply"), None, None),
        P(("shaft", "ply"), None, None),
        P(("shaft", "ply"), None),
    )
    out_specs = (P(None, "ply", "shaft"), P(None, "ply", "shaft"), P(None, "ply", "shaft"))
    return jax.shard_map(
        on_device, mesh=mesh, in_specs=in_specs, out_specs=out_specs, check_vma=False
    )
```

```python
import jax
import jax.numpy as jnp
from jax import lax
from jax.experimental import pallas as pl
from jax.experimental.pallas import tpu as pltpu
from jax.sharding import PartitionSpec as P

ITERS = 4
ROWS = 8


time_step = 0.25


def padded_2(value, sides, width):
    for axis, dim in sides:
        size, length = (lax.axis_size(axis), value.shape[dim])
        up = [(i, (i + 1) % size) for i in range(size - 1)]
        down = [(j, i) for i, j in up]
        last = lax.slice_in_dim(value, length - width, length, axis=dim)
        first = lax.slice_in_dim(value, 0, width, axis=dim)
        before = lax.ppermute(last, axis, up)
        after = lax.ppermute(first, axis, down)
        value = jnp.concatenate([before, value, after], axis=dim)
    return value


def halo(rounded):
    shafts, plies = lax.axis_size("shaft"), lax.axis_size("ply")

    def receive(value, shaft_offset, ply_offset):
        perm = [
            (a * plies + q, (a - shaft_offset) * plies + q - ply_offset)
            for a in range(shafts)
            for q in range(plies)
            if 0 <= a - shaft_offset < shafts and 0 <= q - ply_offset < plies
        ]
        return lax.ppermute(value, ("shaft", "ply"), perm)

    first, last = rounded[:, :1], rounded[:, -1:]
    rows = []
    for ply_offset in (-1, 0, 1):
        middle = rounded if ply_offset == 0 else receive(rounded, 0, ply_offset)
        rows.append(
            jnp.concatenate(
                [receive(last, -1, ply_offset), middle, receive(first, 1, ply_offset)], 1
            )
        )
    return jnp.stack(rows, 1)


def neighbour_exchange(axis, lower_bound, upper_bound):
    size = lax.axis_size(axis)
    up = [(i, i + 1) for i in range(size - 1)]
    down = [(i + 1, i) for i in range(size - 1)]
    from_lower = lax.ppermute(upper_bound, axis, up)
    from_higher = lax.ppermute(lower_bound, axis, down)
    return from_lower, from_higher


def gather_kernel(s_ref, lo_ref, hi_ref, out_lo_ref, out_hi_ref):
    flat = s_ref[0]
    for pick_ref, out_ref in ((lo_ref, out_lo_ref), (hi_ref, out_hi_ref)):
        picked = lax.dot_general(
            pick_ref[...], flat, (((1,), (1,)), ((), ())), preferred_element_type=jnp.float32
        )
        out_ref[0] = picked.astype(out_ref.dtype)


def gather_leaving(stiffness, pick_lo, pick_hi):
    slots, depth, blocks = stiffness.shape
    width = pick_lo.shape[0]
    out = jax.ShapeDtypeStruct((slots, width, depth), stiffness.dtype)
    return pl.pallas_call(
        gather_kernel,
        grid=(slots,),
        in_specs=[
            pl.BlockSpec((1, depth, blocks), lambda k: (k, 0, 0)),
            pl.BlockSpec((width, blocks), lambda k: (0, 0)),
            pl.BlockSpec((width, blocks), lambda k: (0, 0)),
        ],
        out_specs=[
            pl.BlockSpec((1, width, depth), lambda k: (k, 0, 0)),
            pl.BlockSpec((1, width, depth), lambda k: (k, 0, 0)),
        ],
        out_shape=[out, out],
    )(stiffness, pick_lo, pick_hi)


def merge_kernel(s_ref, lo_ref, hi_ref, place_lo_ref, place_hi_ref, arrival_ref, out_ref):
    placed = jnp.dot(
        lo_ref[0].T, place_lo_ref[...], preferred_element_type=jnp.float32
    ) + jnp.dot(hi_ref[0].T, place_hi_ref[...], preferred_element_type=jnp.float32)
    placed = placed.astype(out_ref.dtype).reshape(s_ref.shape[1:])
    out_ref[0] = jnp.where(arrival_ref[...] > 0, placed, s_ref[0])


def merge_arrived(stiffness, arrived_lo, arrived_hi, place_lo, place_hi, arrival):
    slots, rows_i, rows_j, blocks = stiffness.shape
    depth = rows_i * rows_j
    width = arrived_lo.shape[1]
    return pl.pallas_call(
        merge_kernel,
        grid=(slots,),
        in_specs=[
            pl.BlockSpec((1, rows_i, rows_j, blocks), lambda k: (k, 0, 0, 0)),
            pl.BlockSpec((1, width, depth), lambda k: (k, 0, 0)),
            pl.BlockSpec((1, width, depth), lambda k: (k, 0, 0)),
            pl.BlockSpec((width, blocks), lambda k: (0, 0)),
            pl.BlockSpec((width, blocks), lambda k: (0, 0)),
            pl.BlockSpec((1, blocks), lambda k: (0, 0)),
        ],
        out_specs=pl.BlockSpec((1, rows_i, rows_j, blocks), lambda k: (k, 0, 0, 0)),
        out_shape=jax.ShapeDtypeStruct(stiffness.shape, stiffness.dtype),
    )(stiffness, arrived_lo, arrived_hi, place_lo, place_hi, arrival)


def force_kernel(s_ref, n_ref, out_ref):
    slots, rows = s_ref.shape[:2]
    for row in range(rows):
        acc = s_ref[0, row].astype(jnp.float32) * n_ref[0]
        for slot_index in range(1, slots):
            acc = acc + s_ref[slot_index, row].astype(jnp.float32) * n_ref[slot_index]
        out_ref[pl.ds(row, 1), :] = jnp.sum(acc, axis=0, keepdims=True)


def block_force(stiffness, neighbours):
    slots, rows_i, rows_j, blocks = stiffness.shape
    return pl.pallas_call(
        force_kernel,
        grid=(rows_i // ROWS,),
        in_specs=[
            pl.BlockSpec((slots, ROWS, rows_j, blocks), lambda i: (0, i, 0, 0)),
            pl.BlockSpec((slots, rows_j, blocks), lambda i: (0, 0, 0)),
        ],
        out_specs=pl.BlockSpec((ROWS, blocks), lambda i: (i, 0)),
        out_shape=jax.ShapeDtypeStruct((rows_i, blocks), jnp.float32),
        cost_estimate=pl.CostEstimate(
            flops=2 * slots * rows_i * rows_j * blocks,
            bytes_accessed=stiffness.size * 2 + neighbours.size * 4 + rows_i * blocks * 4,
            transcendentals=0,
        ),
    )(stiffness, neighbours)


def on_device(
    displacement,
    velocity,
    external,
    mass_inverse,
    pattern,
    coupled,
    stiffness_old,
    history_old,
    decay_old,
    strain_map,
    send_slot,
    arrive_place,
    arrive_count,
):
    blocks = displacement.shape[-1]
    capacity = send_slot.shape[2]
    slots = stiffness_old.shape[0]
    lanes = jnp.arange(blocks, dtype=jnp.int32)

    slots, rows_i, rows_j, _ = stiffness_old.shape
    stiff_flat = stiffness_old.reshape(slots, rows_i * rows_j, blocks)
    leave_lo = (send_slot[0, 0][:, None] == lanes[None, :]).astype(jnp.bfloat16)
    leave_hi = (send_slot[0, 1][:, None] == lanes[None, :]).astype(jnp.bfloat16)
    stiff_to_lower, stiff_to_higher = gather_leaving(stiff_flat, leave_lo, leave_hi)
    stiff_lower, stiff_higher = neighbour_exchange("shaft", stiff_to_lower, stiff_to_higher)

    count_live = jnp.arange(capacity, dtype=jnp.int32)[None, :] < arrive_count[0][:, None]
    place_lo = (arrive_place[0, 0][:, None] == lanes[None, :]) & count_live[0][:, None]
    place_hi = (arrive_place[0, 1][:, None] == lanes[None, :]) & count_live[1][:, None]
    arrival = (jnp.any(place_lo, 0) | jnp.any(place_hi, 0)).astype(jnp.int32)[None, :]
    stiffness = merge_arrived(
        stiffness_old,
        stiff_lower,
        stiff_higher,
        place_lo.astype(jnp.bfloat16),
        place_hi.astype(jnp.bfloat16),
        arrival,
    )

    outgoing = send_slot[0].reshape(-1)
    filled = count_live.reshape(-1)
    target = jnp.where(filled, arrive_place[0].reshape(-1), blocks)
    placing = (
        jnp.arange(blocks + 1, dtype=jnp.int32)
        .at[target]
        .set(blocks + jnp.arange(2 * capacity, dtype=jnp.int32))[:blocks]
    )
    moving_state = jnp.concatenate(
        [jnp.take(history_old, outgoing, axis=1), jnp.take(decay_old, outgoing, axis=1)], 0
    )
    state_lower, state_higher = neighbour_exchange(
        "shaft", moving_state[:, :capacity], moving_state[:, capacity:]
    )
    state_arrived = jnp.concatenate([state_lower, state_higher], 1)
    depth = history_old.shape[0]
    history = jnp.take(jnp.concatenate([history_old, state_arrived[:depth]], 1), placing, axis=1)
    decay = jnp.take(jnp.concatenate([decay_old, state_arrived[depth:]], 1), placing, axis=1)

    moved = displacement[:, 0, :]
    speeds = velocity[:, 0, :]
    forcing = external[:, 0, :]
    scaling = mass_inverse[:, 0, :]
    live = jnp.arange(slots, dtype=jnp.int32)[:, None] < coupled[0][None, :]
    codes = jnp.where(live, pattern[:, 0, :], 9)[:, None, :]
    for repeat in range(ITERS):
        padded = halo(moved.astype(jnp.bfloat16))
        neighbours = jnp.zeros((slots,) + moved.shape, jnp.bfloat16)
        for code_index in range(9):
            shifted = padded[:, code_index // 3, code_index % 3 : code_index % 3 + blocks]
            neighbours = jnp.where(codes == code_index, shifted[None], neighbours)
        product = stiffness.astype(jnp.float32) * neighbours.astype(jnp.float32)[:, None, :, :]
        force = jnp.sum(product, axis=(0, 2)) + jnp.dot(
            strain_map.T, history, precision=lax.Precision.HIGHEST
        )
        speeds = speeds + time_step * (scaling * (forcing - force))
        advanced = moved + time_step * speeds
        history = decay * history + jnp.dot(
            strain_map, advanced - moved, precision=lax.Precision.HIGHEST
        )
        moved = advanced
    return (moved[:, None, :], speeds[:, None, :], history[:, None, :])


def solution(mesh):
    in_specs = (
        P(None, "ply", "shaft"),
        P(None, "ply", "shaft"),
        P(None, "ply", "shaft"),
        P(None, "ply", "shaft"),
        P(None, "ply", "shaft"),
        P("ply", "shaft"),
        P(None, None, None, ("shaft", "ply")),
        P(None, ("shaft", "ply")),
        P(None, ("shaft", "ply")),
        P(),
        P(("shaft", "ply"), None, None),
        P(("shaft", "ply"), None, None),
        P(("shaft", "ply"), None),
    )
    out_specs = (P(None, "ply", "shaft"), P(None, "ply", "shaft"), P(None, "ply", "shaft"))
    return jax.shard_map(
        on_device, mesh=mesh, in_specs=in_specs, out_specs=out_specs, check_vma=False
    )
```

```python
import jax
import jax.numpy as jnp
from jax import lax
from jax.experimental import pallas as pl
from jax.experimental.pallas import tpu as pltpu
from jax.sharding import PartitionSpec as P

ITERS = 4
ROWS = 8


time_step = 0.25


def padded_2(value, sides, width):
    for axis, dim in sides:
        size, length = (lax.axis_size(axis), value.shape[dim])
        up = [(i, (i + 1) % size) for i in range(size - 1)]
        down = [(j, i) for i, j in up]
        last = lax.slice_in_dim(value, length - width, length, axis=dim)
        first = lax.slice_in_dim(value, 0, width, axis=dim)
        before = lax.ppermute(last, axis, up)
        after = lax.ppermute(first, axis, down)
        value = jnp.concatenate([before, value, after], axis=dim)
    return value


def neighbour_exchange(axis, lower_bound, upper_bound):
    size = lax.axis_size(axis)
    up = [(i, i + 1) for i in range(size - 1)]
    down = [(i + 1, i) for i in range(size - 1)]
    from_lower = lax.ppermute(upper_bound, axis, up)
    from_higher = lax.ppermute(lower_bound, axis, down)
    return from_lower, from_higher


def gather_kernel(s_ref, lo_ref, hi_ref, out_lo_ref, out_hi_ref):
    width = lo_ref.shape[0]
    pick = jnp.concatenate([lo_ref[...], hi_ref[...]], 0)
    picked = lax.dot_general(
        pick, s_ref[0], (((1,), (1,)), ((), ())), preferred_element_type=jnp.float32
    )
    out_lo_ref[0] = picked[:width].astype(out_lo_ref.dtype)
    out_hi_ref[0] = picked[width:].astype(out_hi_ref.dtype)


def gather_leaving(stiffness, pick_lo, pick_hi):
    slots, depth, blocks = stiffness.shape
    width = pick_lo.shape[0]
    out = jax.ShapeDtypeStruct((slots, width, depth), stiffness.dtype)
    return pl.pallas_call(
        gather_kernel,
        grid=(slots,),
        in_specs=[
            pl.BlockSpec((1, depth, blocks), lambda k: (k, 0, 0)),
            pl.BlockSpec((width, blocks), lambda k: (0, 0)),
            pl.BlockSpec((width, blocks), lambda k: (0, 0)),
        ],
        out_specs=[
            pl.BlockSpec((1, width, depth), lambda k: (k, 0, 0)),
            pl.BlockSpec((1, width, depth), lambda k: (k, 0, 0)),
        ],
        out_shape=[out, out],
    )(stiffness, pick_lo, pick_hi)


def merge_kernel(s_ref, lo_ref, hi_ref, place_lo_ref, place_hi_ref, arrival_ref, out_ref):
    arrived = jnp.concatenate([lo_ref[0], hi_ref[0]], 0)
    place = jnp.concatenate([place_lo_ref[...], place_hi_ref[...]], 0)
    placed = jnp.dot(arrived.T, place, preferred_element_type=jnp.float32)
    placed = placed.astype(out_ref.dtype).reshape(s_ref.shape[1:])
    out_ref[0] = jnp.where(arrival_ref[...] > 0, placed, s_ref[0])


def merge_arrived(stiffness, arrived_lo, arrived_hi, place_lo, place_hi, arrival):
    slots, rows_i, rows_j, blocks = stiffness.shape
    depth = rows_i * rows_j
    width = arrived_lo.shape[1]
    return pl.pallas_call(
        merge_kernel,
        grid=(slots,),
        in_specs=[
            pl.BlockSpec((1, rows_i, rows_j, blocks), lambda k: (k, 0, 0, 0)),
            pl.BlockSpec((1, width, depth), lambda k: (k, 0, 0)),
            pl.BlockSpec((1, width, depth), lambda k: (k, 0, 0)),
            pl.BlockSpec((width, blocks), lambda k: (0, 0)),
            pl.BlockSpec((width, blocks), lambda k: (0, 0)),
            pl.BlockSpec((1, blocks), lambda k: (0, 0)),
        ],
        out_specs=pl.BlockSpec((1, rows_i, rows_j, blocks), lambda k: (k, 0, 0, 0)),
        out_shape=jax.ShapeDtypeStruct(stiffness.shape, stiffness.dtype),
    )(stiffness, arrived_lo, arrived_hi, place_lo, place_hi, arrival)


def force_kernel(s_ref, n_ref, out_ref):
    slots, rows = s_ref.shape[:2]
    for row in range(rows):
        acc = s_ref[0, row].astype(jnp.float32) * n_ref[0]
        for slot_index in range(1, slots):
            acc = acc + s_ref[slot_index, row].astype(jnp.float32) * n_ref[slot_index]
        out_ref[pl.ds(row, 1), :] = jnp.sum(acc, axis=0, keepdims=True)


def block_force(stiffness, neighbours):
    slots, rows_i, rows_j, blocks = stiffness.shape
    return pl.pallas_call(
        force_kernel,
        grid=(rows_i // ROWS,),
        in_specs=[
            pl.BlockSpec((slots, ROWS, rows_j, blocks), lambda i: (0, i, 0, 0)),
            pl.BlockSpec((slots, rows_j, blocks), lambda i: (0, 0, 0)),
        ],
        out_specs=pl.BlockSpec((ROWS, blocks), lambda i: (i, 0)),
        out_shape=jax.ShapeDtypeStruct((rows_i, blocks), jnp.float32),
        cost_estimate=pl.CostEstimate(
            flops=2 * slots * rows_i * rows_j * blocks,
            bytes_accessed=stiffness.size * 2 + neighbours.size * 4 + rows_i * blocks * 4,
            transcendentals=0,
        ),
    )(stiffness, neighbours)


def on_device(
    displacement,
    velocity,
    external,
    mass_inverse,
    pattern,
    coupled,
    stiffness_old,
    history_old,
    decay_old,
    strain_map,
    send_slot,
    arrive_place,
    arrive_count,
):
    blocks = displacement.shape[-1]
    capacity = send_slot.shape[2]
    slots = stiffness_old.shape[0]
    lanes = jnp.arange(blocks, dtype=jnp.int32)

    slots, rows_i, rows_j, _ = stiffness_old.shape
    stiff_flat = stiffness_old.reshape(slots, rows_i * rows_j, blocks)
    leave_lo = (send_slot[0, 0][:, None] == lanes[None, :]).astype(jnp.bfloat16)
    leave_hi = (send_slot[0, 1][:, None] == lanes[None, :]).astype(jnp.bfloat16)
    stiff_to_lower, stiff_to_higher = gather_leaving(stiff_flat, leave_lo, leave_hi)
    stiff_lower, stiff_higher = neighbour_exchange("shaft", stiff_to_lower, stiff_to_higher)

    count_live = jnp.arange(capacity, dtype=jnp.int32)[None, :] < arrive_count[0][:, None]
    place_lo = (arrive_place[0, 0][:, None] == lanes[None, :]) & count_live[0][:, None]
    place_hi = (arrive_place[0, 1][:, None] == lanes[None, :]) & count_live[1][:, None]
    arrival = (jnp.any(place_lo, 0) | jnp.any(place_hi, 0)).astype(jnp.int32)[None, :]
    stiffness = merge_arrived(
        stiffness_old,
        stiff_lower,
        stiff_higher,
        place_lo.astype(jnp.bfloat16),
        place_hi.astype(jnp.bfloat16),
        arrival,
    )

    outgoing = send_slot[0].reshape(-1)
    filled = count_live.reshape(-1)
    target = jnp.where(filled, arrive_place[0].reshape(-1), blocks)
    placing = (
        jnp.arange(blocks + 1, dtype=jnp.int32)
        .at[target]
        .set(blocks + jnp.arange(2 * capacity, dtype=jnp.int32))[:blocks]
    )
    moving_state = jnp.concatenate(
        [jnp.take(history_old, outgoing, axis=1), jnp.take(decay_old, outgoing, axis=1)], 0
    )
    state_lower, state_higher = neighbour_exchange(
        "shaft", moving_state[:, :capacity], moving_state[:, capacity:]
    )
    state_arrived = jnp.concatenate([state_lower, state_higher], 1)
    depth = history_old.shape[0]
    history = jnp.take(jnp.concatenate([history_old, state_arrived[:depth]], 1), placing, axis=1)
    decay = jnp.take(jnp.concatenate([decay_old, state_arrived[depth:]], 1), placing, axis=1)

    moved = displacement[:, 0, :]
    speeds = velocity[:, 0, :]
    forcing = external[:, 0, :]
    scaling = mass_inverse[:, 0, :]
    live = jnp.arange(slots, dtype=jnp.int32)[:, None] < coupled[0][None, :]
    codes = jnp.where(live, pattern[:, 0, :], 9)[:, None, :]
    for repeat in range(ITERS):
        rounded = moved.astype(jnp.bfloat16)[:, None, :]
        padded = padded_2(rounded, (("shaft", 2), ("ply", 1)), 1)
        neighbours = jnp.zeros((slots,) + moved.shape, jnp.bfloat16)
        for code_index in range(9):
            shifted = padded[:, code_index // 3, code_index % 3 : code_index % 3 + blocks]
            neighbours = jnp.where(codes == code_index, shifted[None], neighbours)
        product = stiffness.astype(jnp.float32) * neighbours.astype(jnp.float32)[:, None, :, :]
        force = jnp.sum(product, axis=(0, 2)) + jnp.dot(
            strain_map.T, history, precision=lax.Precision.HIGHEST
        )
        speeds = speeds + time_step * (scaling * (forcing - force))
        advanced = moved + time_step * speeds
        history = decay * history + jnp.dot(
            strain_map, advanced - moved, precision=lax.Precision.HIGHEST
        )
        moved = advanced
    return (moved[:, None, :], speeds[:, None, :], history[:, None, :])


def solution(mesh):
    in_specs = (
        P(None, "ply", "shaft"),
        P(None, "ply", "shaft"),
        P(None, "ply", "shaft"),
        P(None, "ply", "shaft"),
        P(None, "ply", "shaft"),
        P("ply", "shaft"),
        P(None, None, None, ("shaft", "ply")),
        P(None, ("shaft", "ply")),
        P(None, ("shaft", "ply")),
        P(),
        P(("shaft", "ply"), None, None),
        P(("shaft", "ply"), None, None),
        P(("shaft", "ply"), None),
    )
    out_specs = (P(None, "ply", "shaft"), P(None, "ply", "shaft"), P(None, "ply", "shaft"))
    return jax.shard_map(
        on_device, mesh=mesh, in_specs=in_specs, out_specs=out_specs, check_vma=False
    )
```

```python
import jax
import jax.numpy as jnp
from jax import lax
from jax.experimental import pallas as pl
from jax.experimental.pallas import tpu as pltpu
from jax.sharding import PartitionSpec as P

ITERS = 4
ROWS = 8


time_step = 0.25


def padded_2(value, sides, width):
    for axis, dim in sides:
        size, length = (lax.axis_size(axis), value.shape[dim])
        up = [(i, (i + 1) % size) for i in range(size - 1)]
        down = [(j, i) for i, j in up]
        last = lax.slice_in_dim(value, length - width, length, axis=dim)
        first = lax.slice_in_dim(value, 0, width, axis=dim)
        before = lax.ppermute(last, axis, up)
        after = lax.ppermute(first, axis, down)
        value = jnp.concatenate([before, value, after], axis=dim)
    return value


def neighbour_exchange(axis, lower_bound, upper_bound):
    size = lax.axis_size(axis)
    up = [(i, i + 1) for i in range(size - 1)]
    down = [(i + 1, i) for i in range(size - 1)]
    from_lower = lax.ppermute(upper_bound, axis, up)
    from_higher = lax.ppermute(lower_bound, axis, down)
    return from_lower, from_higher


def gather_kernel(s_ref, lo_ref, hi_ref, out_lo_ref, out_hi_ref):
    width = lo_ref.shape[0]
    pick = jnp.concatenate([lo_ref[...], hi_ref[...]], 0)
    picked = lax.dot_general(
        pick, s_ref[0], (((1,), (1,)), ((), ())), preferred_element_type=jnp.float32
    )
    out_lo_ref[0] = picked[:width].astype(out_lo_ref.dtype)
    out_hi_ref[0] = picked[width:].astype(out_hi_ref.dtype)


def gather_leaving(stiffness, pick_lo, pick_hi):
    slots, depth, blocks = stiffness.shape
    width = pick_lo.shape[0]
    out = jax.ShapeDtypeStruct((slots, width, depth), stiffness.dtype)
    return pl.pallas_call(
        gather_kernel,
        grid=(slots,),
        in_specs=[
            pl.BlockSpec((1, depth, blocks), lambda k: (k, 0, 0)),
            pl.BlockSpec((width, blocks), lambda k: (0, 0)),
            pl.BlockSpec((width, blocks), lambda k: (0, 0)),
        ],
        out_specs=[
            pl.BlockSpec((1, width, depth), lambda k: (k, 0, 0)),
            pl.BlockSpec((1, width, depth), lambda k: (k, 0, 0)),
        ],
        out_shape=[out, out],
    )(stiffness, pick_lo, pick_hi)


def merge_kernel(s_ref, lo_ref, hi_ref, place_lo_ref, place_hi_ref, arrival_ref, out_ref):
    arrived = jnp.concatenate([lo_ref[0], hi_ref[0]], 0)
    place = jnp.concatenate([place_lo_ref[...], place_hi_ref[...]], 0)
    placed = jnp.dot(arrived.T, place, preferred_element_type=jnp.float32)
    placed = placed.astype(out_ref.dtype).reshape(s_ref.shape[1:])
    out_ref[0] = jnp.where(arrival_ref[...] > 0, placed, s_ref[0])


def merge_arrived(stiffness, arrived_lo, arrived_hi, place_lo, place_hi, arrival):
    slots, rows_i, rows_j, blocks = stiffness.shape
    depth = rows_i * rows_j
    width = arrived_lo.shape[1]
    return pl.pallas_call(
        merge_kernel,
        grid=(slots,),
        in_specs=[
            pl.BlockSpec((1, rows_i, rows_j, blocks), lambda k: (k, 0, 0, 0)),
            pl.BlockSpec((1, width, depth), lambda k: (k, 0, 0)),
            pl.BlockSpec((1, width, depth), lambda k: (k, 0, 0)),
            pl.BlockSpec((width, blocks), lambda k: (0, 0)),
            pl.BlockSpec((width, blocks), lambda k: (0, 0)),
            pl.BlockSpec((1, blocks), lambda k: (0, 0)),
        ],
        out_specs=pl.BlockSpec((1, rows_i, rows_j, blocks), lambda k: (k, 0, 0, 0)),
        out_shape=jax.ShapeDtypeStruct(stiffness.shape, stiffness.dtype),
    )(stiffness, arrived_lo, arrived_hi, place_lo, place_hi, arrival)


def force_kernel(s_ref, n_ref, out_ref):
    slots, rows = s_ref.shape[:2]
    for row in range(rows):
        acc = s_ref[0, row].astype(jnp.float32) * n_ref[0]
        for slot_index in range(1, slots):
            acc = acc + s_ref[slot_index, row].astype(jnp.float32) * n_ref[slot_index]
        out_ref[pl.ds(row, 1), :] = jnp.sum(acc, axis=0, keepdims=True)


def block_force(stiffness, neighbours):
    slots, rows_i, rows_j, blocks = stiffness.shape
    return pl.pallas_call(
        force_kernel,
        grid=(rows_i // ROWS,),
        in_specs=[
            pl.BlockSpec((slots, ROWS, rows_j, blocks), lambda i: (0, i, 0, 0)),
            pl.BlockSpec((slots, rows_j, blocks), lambda i: (0, 0, 0)),
        ],
        out_specs=pl.BlockSpec((ROWS, blocks), lambda i: (i, 0)),
        out_shape=jax.ShapeDtypeStruct((rows_i, blocks), jnp.float32),
        cost_estimate=pl.CostEstimate(
            flops=2 * slots * rows_i * rows_j * blocks,
            bytes_accessed=stiffness.size * 2 + neighbours.size * 4 + rows_i * blocks * 4,
            transcendentals=0,
        ),
    )(stiffness, neighbours)


def on_device(
    displacement,
    velocity,
    external,
    mass_inverse,
    pattern,
    coupled,
    stiffness_old,
    history_old,
    decay_old,
    strain_map,
    send_slot,
    arrive_place,
    arrive_count,
):
    blocks = displacement.shape[-1]
    capacity = send_slot.shape[2]
    slots = stiffness_old.shape[0]
    lanes = jnp.arange(blocks, dtype=jnp.int32)

    slots, rows_i, rows_j, _ = stiffness_old.shape
    stiff_flat = stiffness_old.reshape(slots, rows_i * rows_j, blocks)
    leave_lo = (send_slot[0, 0][:, None] == lanes[None, :]).astype(jnp.bfloat16)
    leave_hi = (send_slot[0, 1][:, None] == lanes[None, :]).astype(jnp.bfloat16)
    stiff_to_lower, stiff_to_higher = gather_leaving(stiff_flat, leave_lo, leave_hi)
    stiff_lower, stiff_higher = neighbour_exchange("shaft", stiff_to_lower, stiff_to_higher)

    count_live = jnp.arange(capacity, dtype=jnp.int32)[None, :] < arrive_count[0][:, None]
    place_lo = (arrive_place[0, 0][:, None] == lanes[None, :]) & count_live[0][:, None]
    place_hi = (arrive_place[0, 1][:, None] == lanes[None, :]) & count_live[1][:, None]
    arrival = (jnp.any(place_lo, 0) | jnp.any(place_hi, 0)).astype(jnp.int32)[None, :]
    stiffness = merge_arrived(
        stiffness_old,
        stiff_lower,
        stiff_higher,
        place_lo.astype(jnp.bfloat16),
        place_hi.astype(jnp.bfloat16),
        arrival,
    )

    place_all = jnp.concatenate([place_lo, place_hi], 0)
    arrived_all = jnp.concatenate([stiff_lower, stiff_higher], 1)
    rows_i, rows_j = stiffness_old.shape[1:3]
    segments = (
        jnp.arange(rows_i * rows_j, dtype=jnp.int32)[:, None] // rows_j
        == jnp.arange(rows_i, dtype=jnp.int32)[None, :]
    ).astype(jnp.float32)

    def first_force(neighbours):
        own = jnp.sum(
            stiffness_old.astype(jnp.float32) * neighbours.astype(jnp.float32)[:, None, :, :],
            axis=(0, 2),
        )
        picked = jnp.einsum(
            "kjb,mb->kmj", neighbours, place_all.astype(jnp.bfloat16),
            preferred_element_type=jnp.float32,
        )
        spread = jnp.tile(picked, (1, 1, rows_i))
        partial = jnp.sum(arrived_all.astype(jnp.float32) * spread, axis=0)
        per_block = jnp.dot(partial, segments, precision=lax.Precision.HIGHEST)
        placed = jnp.dot(
            per_block.T, place_all.astype(jnp.float32), precision=lax.Precision.HIGHEST
        )
        return jnp.where(arrival > 0, placed, own)

    outgoing = send_slot[0].reshape(-1)
    filled = count_live.reshape(-1)
    target = jnp.where(filled, arrive_place[0].reshape(-1), blocks)
    placing = (
        jnp.arange(blocks + 1, dtype=jnp.int32)
        .at[target]
        .set(blocks + jnp.arange(2 * capacity, dtype=jnp.int32))[:blocks]
    )
    moving_state = jnp.concatenate(
        [jnp.take(history_old, outgoing, axis=1), jnp.take(decay_old, outgoing, axis=1)], 0
    )
    state_lower, state_higher = neighbour_exchange(
        "shaft", moving_state[:, :capacity], moving_state[:, capacity:]
    )
    state_arrived = jnp.concatenate([state_lower, state_higher], 1)
    depth = history_old.shape[0]
    history = jnp.take(jnp.concatenate([history_old, state_arrived[:depth]], 1), placing, axis=1)
    decay = jnp.take(jnp.concatenate([decay_old, state_arrived[depth:]], 1), placing, axis=1)

    moved = displacement[:, 0, :]
    speeds = velocity[:, 0, :]
    forcing = external[:, 0, :]
    scaling = mass_inverse[:, 0, :]
    live = jnp.arange(slots, dtype=jnp.int32)[:, None] < coupled[0][None, :]
    codes = jnp.where(live, pattern[:, 0, :], 9)[:, None, :]
    for repeat in range(ITERS):
        rounded = moved.astype(jnp.bfloat16)[:, None, :]
        padded = padded_2(rounded, (("shaft", 2), ("ply", 1)), 1)
        neighbours = jnp.zeros((slots,) + moved.shape, jnp.bfloat16)
        for code_index in range(9):
            shifted = padded[:, code_index // 3, code_index % 3 : code_index % 3 + blocks]
            neighbours = jnp.where(codes == code_index, shifted[None], neighbours)
        if repeat == 0:
            force = first_force(neighbours) + jnp.dot(
                strain_map.T, history, precision=lax.Precision.HIGHEST
            )
        else:
            product = stiffness.astype(jnp.float32) * neighbours.astype(jnp.float32)[:, None, :, :]
            force = jnp.sum(product, axis=(0, 2)) + jnp.dot(
                strain_map.T, history, precision=lax.Precision.HIGHEST
            )
        speeds = speeds + time_step * (scaling * (forcing - force))
        advanced = moved + time_step * speeds
        history = decay * history + jnp.dot(
            strain_map, advanced - moved, precision=lax.Precision.HIGHEST
        )
        moved = advanced
    return (moved[:, None, :], speeds[:, None, :], history[:, None, :])


def solution(mesh):
    in_specs = (
        P(None, "ply", "shaft"),
        P(None, "ply", "shaft"),
        P(None, "ply", "shaft"),
        P(None, "ply", "shaft"),
        P(None, "ply", "shaft"),
        P("ply", "shaft"),
        P(None, None, None, ("shaft", "ply")),
        P(None, ("shaft", "ply")),
        P(None, ("shaft", "ply")),
        P(),
        P(("shaft", "ply"), None, None),
        P(("shaft", "ply"), None, None),
        P(("shaft", "ply"), None),
    )
    out_specs = (P(None, "ply", "shaft"), P(None, "ply", "shaft"), P(None, "ply", "shaft"))
    return jax.shard_map(
        on_device, mesh=mesh, in_specs=in_specs, out_specs=out_specs, check_vma=False
    )
```

```python
import jax
import jax.numpy as jnp
from jax import lax
from jax.experimental import pallas as pl
from jax.experimental.pallas import tpu as pltpu
from jax.sharding import PartitionSpec as P

ITERS = 4
ROWS = 8


time_step = 0.25


def padded_2(value, sides, width):
    for axis, dim in sides:
        size, length = (lax.axis_size(axis), value.shape[dim])
        up = [(i, (i + 1) % size) for i in range(size - 1)]
        down = [(j, i) for i, j in up]
        last = lax.slice_in_dim(value, length - width, length, axis=dim)
        first = lax.slice_in_dim(value, 0, width, axis=dim)
        before = lax.ppermute(last, axis, up)
        after = lax.ppermute(first, axis, down)
        value = jnp.concatenate([before, value, after], axis=dim)
    return value


def neighbour_exchange(axis, lower_bound, upper_bound):
    size = lax.axis_size(axis)
    up = [(i, i + 1) for i in range(size - 1)]
    down = [(i + 1, i) for i in range(size - 1)]
    from_lower = lax.ppermute(upper_bound, axis, up)
    from_higher = lax.ppermute(lower_bound, axis, down)
    return from_lower, from_higher


def gather_kernel(s_ref, lo_ref, hi_ref, out_lo_ref, out_hi_ref):
    width = lo_ref.shape[0]
    pick = jnp.concatenate([lo_ref[...], hi_ref[...]], 0)
    picked = lax.dot_general(
        pick, s_ref[0], (((1,), (1,)), ((), ())), preferred_element_type=jnp.float32
    )
    out_lo_ref[0] = picked[:width].astype(out_lo_ref.dtype)
    out_hi_ref[0] = picked[width:].astype(out_hi_ref.dtype)


def gather_leaving(stiffness, pick_lo, pick_hi):
    slots, depth, blocks = stiffness.shape
    width = pick_lo.shape[0]
    out = jax.ShapeDtypeStruct((slots, width, depth), stiffness.dtype)
    return pl.pallas_call(
        gather_kernel,
        grid=(slots,),
        in_specs=[
            pl.BlockSpec((1, depth, blocks), lambda k: (k, 0, 0)),
            pl.BlockSpec((width, blocks), lambda k: (0, 0)),
            pl.BlockSpec((width, blocks), lambda k: (0, 0)),
        ],
        out_specs=[
            pl.BlockSpec((1, width, depth), lambda k: (k, 0, 0)),
            pl.BlockSpec((1, width, depth), lambda k: (k, 0, 0)),
        ],
        out_shape=[out, out],
    )(stiffness, pick_lo, pick_hi)


def merge_kernel(s_ref, lo_ref, hi_ref, place_lo_ref, place_hi_ref, arrival_ref, out_ref):
    arrived = jnp.concatenate([lo_ref[0], hi_ref[0]], 0)
    place = jnp.concatenate([place_lo_ref[...], place_hi_ref[...]], 0)
    placed = jnp.dot(arrived.T, place, preferred_element_type=jnp.float32)
    placed = placed.astype(out_ref.dtype).reshape(s_ref.shape[1:])
    out_ref[0] = jnp.where(arrival_ref[...] > 0, placed, s_ref[0])


def merge_arrived(stiffness, arrived_lo, arrived_hi, place_lo, place_hi, arrival):
    slots, rows_i, rows_j, blocks = stiffness.shape
    depth = rows_i * rows_j
    width = arrived_lo.shape[1]
    return pl.pallas_call(
        merge_kernel,
        grid=(slots,),
        in_specs=[
            pl.BlockSpec((1, rows_i, rows_j, blocks), lambda k: (k, 0, 0, 0)),
            pl.BlockSpec((1, width, depth), lambda k: (k, 0, 0)),
            pl.BlockSpec((1, width, depth), lambda k: (k, 0, 0)),
            pl.BlockSpec((width, blocks), lambda k: (0, 0)),
            pl.BlockSpec((width, blocks), lambda k: (0, 0)),
            pl.BlockSpec((1, blocks), lambda k: (0, 0)),
        ],
        out_specs=pl.BlockSpec((1, rows_i, rows_j, blocks), lambda k: (k, 0, 0, 0)),
        out_shape=jax.ShapeDtypeStruct(stiffness.shape, stiffness.dtype),
    )(stiffness, arrived_lo, arrived_hi, place_lo, place_hi, arrival)


def force_kernel(s_ref, n_ref, out_ref):
    slots, rows = s_ref.shape[:2]
    for row in range(rows):
        acc = s_ref[0, row].astype(jnp.float32) * n_ref[0]
        for slot_index in range(1, slots):
            acc = acc + s_ref[slot_index, row].astype(jnp.float32) * n_ref[slot_index]
        out_ref[pl.ds(row, 1), :] = jnp.sum(acc, axis=0, keepdims=True)


def block_force(stiffness, neighbours):
    slots, rows_i, rows_j, blocks = stiffness.shape
    return pl.pallas_call(
        force_kernel,
        grid=(rows_i // ROWS,),
        in_specs=[
            pl.BlockSpec((slots, ROWS, rows_j, blocks), lambda i: (0, i, 0, 0)),
            pl.BlockSpec((slots, rows_j, blocks), lambda i: (0, 0, 0)),
        ],
        out_specs=pl.BlockSpec((ROWS, blocks), lambda i: (i, 0)),
        out_shape=jax.ShapeDtypeStruct((rows_i, blocks), jnp.float32),
        cost_estimate=pl.CostEstimate(
            flops=2 * slots * rows_i * rows_j * blocks,
            bytes_accessed=stiffness.size * 2 + neighbours.size * 4 + rows_i * blocks * 4,
            transcendentals=0,
        ),
    )(stiffness, neighbours)


def on_device(
    displacement,
    velocity,
    external,
    mass_inverse,
    pattern,
    coupled,
    stiffness_old,
    history_old,
    decay_old,
    strain_map,
    send_slot,
    arrive_place,
    arrive_count,
):
    blocks = displacement.shape[-1]
    capacity = send_slot.shape[2]
    slots = stiffness_old.shape[0]
    lanes = jnp.arange(blocks, dtype=jnp.int32)

    slots, rows_i, rows_j, _ = stiffness_old.shape
    stiff_flat = stiffness_old.reshape(slots, rows_i * rows_j, blocks)
    leave_lo = (send_slot[0, 0][:, None] == lanes[None, :]).astype(jnp.bfloat16)
    leave_hi = (send_slot[0, 1][:, None] == lanes[None, :]).astype(jnp.bfloat16)
    stiff_to_lower, stiff_to_higher = gather_leaving(stiff_flat, leave_lo, leave_hi)
    cut = (slots + 1) // 2
    pieces = [
        neighbour_exchange("shaft", stiff_to_lower[part], stiff_to_higher[part])
        for part in (slice(0, cut), slice(cut, slots))
    ]
    stiff_lower = jnp.concatenate([piece[0] for piece in pieces], 0)
    stiff_higher = jnp.concatenate([piece[1] for piece in pieces], 0)

    count_live = jnp.arange(capacity, dtype=jnp.int32)[None, :] < arrive_count[0][:, None]
    place_lo = (arrive_place[0, 0][:, None] == lanes[None, :]) & count_live[0][:, None]
    place_hi = (arrive_place[0, 1][:, None] == lanes[None, :]) & count_live[1][:, None]
    arrival = (jnp.any(place_lo, 0) | jnp.any(place_hi, 0)).astype(jnp.int32)[None, :]
    stiffness = merge_arrived(
        stiffness_old,
        stiff_lower,
        stiff_higher,
        place_lo.astype(jnp.bfloat16),
        place_hi.astype(jnp.bfloat16),
        arrival,
    )

    outgoing = send_slot[0].reshape(-1)
    filled = count_live.reshape(-1)
    target = jnp.where(filled, arrive_place[0].reshape(-1), blocks)
    placing = (
        jnp.arange(blocks + 1, dtype=jnp.int32)
        .at[target]
        .set(blocks + jnp.arange(2 * capacity, dtype=jnp.int32))[:blocks]
    )
    moving_state = jnp.concatenate(
        [jnp.take(history_old, outgoing, axis=1), jnp.take(decay_old, outgoing, axis=1)], 0
    )
    state_lower, state_higher = neighbour_exchange(
        "shaft", moving_state[:, :capacity], moving_state[:, capacity:]
    )
    state_arrived = jnp.concatenate([state_lower, state_higher], 1)
    depth = history_old.shape[0]
    history = jnp.take(jnp.concatenate([history_old, state_arrived[:depth]], 1), placing, axis=1)
    decay = jnp.take(jnp.concatenate([decay_old, state_arrived[depth:]], 1), placing, axis=1)

    moved = displacement[:, 0, :]
    speeds = velocity[:, 0, :]
    forcing = external[:, 0, :]
    scaling = mass_inverse[:, 0, :]
    live = jnp.arange(slots, dtype=jnp.int32)[:, None] < coupled[0][None, :]
    codes = jnp.where(live, pattern[:, 0, :], 9)[:, None, :]
    for repeat in range(ITERS):
        rounded = moved.astype(jnp.bfloat16)[:, None, :]
        padded = padded_2(rounded, (("shaft", 2), ("ply", 1)), 1)
        neighbours = jnp.zeros((slots,) + moved.shape, jnp.bfloat16)
        for code_index in range(9):
            shifted = padded[:, code_index // 3, code_index % 3 : code_index % 3 + blocks]
            neighbours = jnp.where(codes == code_index, shifted[None], neighbours)
        product = stiffness.astype(jnp.float32) * neighbours.astype(jnp.float32)[:, None, :, :]
        force = jnp.sum(product, axis=(0, 2)) + jnp.dot(
            strain_map.T, history, precision=lax.Precision.HIGHEST
        )
        speeds = speeds + time_step * (scaling * (forcing - force))
        advanced = moved + time_step * speeds
        history = decay * history + jnp.dot(
            strain_map, advanced - moved, precision=lax.Precision.HIGHEST
        )
        moved = advanced
    return (moved[:, None, :], speeds[:, None, :], history[:, None, :])


def solution(mesh):
    in_specs = (
        P(None, "ply", "shaft"),
        P(None, "ply", "shaft"),
        P(None, "ply", "shaft"),
        P(None, "ply", "shaft"),
        P(None, "ply", "shaft"),
        P("ply", "shaft"),
        P(None, None, None, ("shaft", "ply")),
        P(None, ("shaft", "ply")),
        P(None, ("shaft", "ply")),
        P(),
        P(("shaft", "ply"), None, None),
        P(("shaft", "ply"), None, None),
        P(("shaft", "ply"), None),
    )
    out_specs = (P(None, "ply", "shaft"), P(None, "ply", "shaft"), P(None, "ply", "shaft"))
    return jax.shard_map(
        on_device, mesh=mesh, in_specs=in_specs, out_specs=out_specs, check_vma=False
    )
```

```python
import jax
import jax.numpy as jnp
from jax import lax
from jax.experimental import pallas as pl
from jax.experimental.pallas import tpu as pltpu
from jax.sharding import PartitionSpec as P

ITERS = 4
ROWS = 8


time_step = 0.25


def padded_2(value, sides, width):
    for axis, dim in sides:
        size, length = (lax.axis_size(axis), value.shape[dim])
        up = [(i, (i + 1) % size) for i in range(size - 1)]
        down = [(j, i) for i, j in up]
        last = lax.slice_in_dim(value, length - width, length, axis=dim)
        first = lax.slice_in_dim(value, 0, width, axis=dim)
        before = lax.ppermute(last, axis, up)
        after = lax.ppermute(first, axis, down)
        value = jnp.concatenate([before, value, after], axis=dim)
    return value


def neighbour_exchange(axis, lower_bound, upper_bound):
    size = lax.axis_size(axis)
    up = [(i, i + 1) for i in range(size - 1)]
    down = [(i + 1, i) for i in range(size - 1)]
    from_lower = lax.ppermute(upper_bound, axis, up)
    from_higher = lax.ppermute(lower_bound, axis, down)
    return from_lower, from_higher


def gather_kernel(s_ref, lo_ref, hi_ref, out_lo_ref, out_hi_ref):
    width = lo_ref.shape[0]
    pick = jnp.concatenate([lo_ref[...], hi_ref[...]], 0)
    picked = lax.dot_general(
        pick, s_ref[0], (((1,), (1,)), ((), ())), preferred_element_type=jnp.float32
    )
    out_lo_ref[0] = picked[:width].astype(out_lo_ref.dtype)
    out_hi_ref[0] = picked[width:].astype(out_hi_ref.dtype)


def gather_leaving(stiffness, pick_lo, pick_hi):
    slots, depth, blocks = stiffness.shape
    width = pick_lo.shape[0]
    out = jax.ShapeDtypeStruct((slots, width, depth), stiffness.dtype)
    return pl.pallas_call(
        gather_kernel,
        grid=(slots,),
        in_specs=[
            pl.BlockSpec((1, depth, blocks), lambda k: (k, 0, 0)),
            pl.BlockSpec((width, blocks), lambda k: (0, 0)),
            pl.BlockSpec((width, blocks), lambda k: (0, 0)),
        ],
        out_specs=[
            pl.BlockSpec((1, width, depth), lambda k: (k, 0, 0)),
            pl.BlockSpec((1, width, depth), lambda k: (k, 0, 0)),
        ],
        out_shape=[out, out],
    )(stiffness, pick_lo, pick_hi)


def merge_kernel(s_ref, lo_ref, hi_ref, place_lo_ref, place_hi_ref, arrival_ref, out_ref):
    arrived = jnp.concatenate([lo_ref[0], hi_ref[0]], 0)
    place = jnp.concatenate([place_lo_ref[...], place_hi_ref[...]], 0)
    placed = jnp.dot(arrived.T, place, preferred_element_type=jnp.float32)
    placed = placed.astype(out_ref.dtype).reshape(s_ref.shape[1:])
    out_ref[0] = jnp.where(arrival_ref[...] > 0, placed, s_ref[0])


def merge_arrived(stiffness, arrived_lo, arrived_hi, place_lo, place_hi, arrival):
    slots, rows_i, rows_j, blocks = stiffness.shape
    depth = rows_i * rows_j
    width = arrived_lo.shape[1]
    return pl.pallas_call(
        merge_kernel,
        grid=(slots,),
        in_specs=[
            pl.BlockSpec((1, rows_i, rows_j, blocks), lambda k: (k, 0, 0, 0)),
            pl.BlockSpec((1, width, depth), lambda k: (k, 0, 0)),
            pl.BlockSpec((1, width, depth), lambda k: (k, 0, 0)),
            pl.BlockSpec((width, blocks), lambda k: (0, 0)),
            pl.BlockSpec((width, blocks), lambda k: (0, 0)),
            pl.BlockSpec((1, blocks), lambda k: (0, 0)),
        ],
        out_specs=pl.BlockSpec((1, rows_i, rows_j, blocks), lambda k: (k, 0, 0, 0)),
        out_shape=jax.ShapeDtypeStruct(stiffness.shape, stiffness.dtype),
    )(stiffness, arrived_lo, arrived_hi, place_lo, place_hi, arrival)


def force_kernel(s_ref, n_ref, out_ref):
    slots, rows = s_ref.shape[:2]
    for row in range(rows):
        acc = s_ref[0, row].astype(jnp.float32) * n_ref[0]
        for slot_index in range(1, slots):
            acc = acc + s_ref[slot_index, row].astype(jnp.float32) * n_ref[slot_index]
        out_ref[pl.ds(row, 1), :] = jnp.sum(acc, axis=0, keepdims=True)


def block_force(stiffness, neighbours):
    slots, rows_i, rows_j, blocks = stiffness.shape
    return pl.pallas_call(
        force_kernel,
        grid=(rows_i // ROWS,),
        in_specs=[
            pl.BlockSpec((slots, ROWS, rows_j, blocks), lambda i: (0, i, 0, 0)),
            pl.BlockSpec((slots, rows_j, blocks), lambda i: (0, 0, 0)),
        ],
        out_specs=pl.BlockSpec((ROWS, blocks), lambda i: (i, 0)),
        out_shape=jax.ShapeDtypeStruct((rows_i, blocks), jnp.float32),
        cost_estimate=pl.CostEstimate(
            flops=2 * slots * rows_i * rows_j * blocks,
            bytes_accessed=stiffness.size * 2 + neighbours.size * 4 + rows_i * blocks * 4,
            transcendentals=0,
        ),
    )(stiffness, neighbours)


def on_device(
    displacement,
    velocity,
    external,
    mass_inverse,
    pattern,
    coupled,
    stiffness_old,
    history_old,
    decay_old,
    strain_map,
    send_slot,
    arrive_place,
    arrive_count,
):
    blocks = displacement.shape[-1]
    capacity = send_slot.shape[2]
    slots = stiffness_old.shape[0]
    lanes = jnp.arange(blocks, dtype=jnp.int32)

    slots, rows_i, rows_j, _ = stiffness_old.shape
    stiff_flat = stiffness_old.reshape(slots, rows_i * rows_j, blocks)
    leave_lo = (send_slot[0, 0][:, None] == lanes[None, :]).astype(jnp.bfloat16)
    leave_hi = (send_slot[0, 1][:, None] == lanes[None, :]).astype(jnp.bfloat16)
    stiff_to_lower, stiff_to_higher = gather_leaving(stiff_flat, leave_lo, leave_hi)
    shaft_first = padded_2(displacement[:, :1, :].astype(jnp.bfloat16), (("shaft", 2),), 1)
    stiff_to_lower, stiff_to_higher, shaft_first = lax.optimization_barrier(
        (stiff_to_lower, stiff_to_higher, shaft_first)
    )
    stiff_lower, stiff_higher = neighbour_exchange("shaft", stiff_to_lower, stiff_to_higher)

    count_live = jnp.arange(capacity, dtype=jnp.int32)[None, :] < arrive_count[0][:, None]
    place_lo = (arrive_place[0, 0][:, None] == lanes[None, :]) & count_live[0][:, None]
    place_hi = (arrive_place[0, 1][:, None] == lanes[None, :]) & count_live[1][:, None]
    arrival = (jnp.any(place_lo, 0) | jnp.any(place_hi, 0)).astype(jnp.int32)[None, :]
    stiffness = merge_arrived(
        stiffness_old,
        stiff_lower,
        stiff_higher,
        place_lo.astype(jnp.bfloat16),
        place_hi.astype(jnp.bfloat16),
        arrival,
    )

    outgoing = send_slot[0].reshape(-1)
    filled = count_live.reshape(-1)
    target = jnp.where(filled, arrive_place[0].reshape(-1), blocks)
    placing = (
        jnp.arange(blocks + 1, dtype=jnp.int32)
        .at[target]
        .set(blocks + jnp.arange(2 * capacity, dtype=jnp.int32))[:blocks]
    )
    moving_state = jnp.concatenate(
        [jnp.take(history_old, outgoing, axis=1), jnp.take(decay_old, outgoing, axis=1)], 0
    )
    state_lower, state_higher = neighbour_exchange(
        "shaft", moving_state[:, :capacity], moving_state[:, capacity:]
    )
    state_arrived = jnp.concatenate([state_lower, state_higher], 1)
    depth = history_old.shape[0]
    history = jnp.take(jnp.concatenate([history_old, state_arrived[:depth]], 1), placing, axis=1)
    decay = jnp.take(jnp.concatenate([decay_old, state_arrived[depth:]], 1), placing, axis=1)

    moved = displacement[:, 0, :]
    speeds = velocity[:, 0, :]
    forcing = external[:, 0, :]
    scaling = mass_inverse[:, 0, :]
    live = jnp.arange(slots, dtype=jnp.int32)[:, None] < coupled[0][None, :]
    codes = jnp.where(live, pattern[:, 0, :], 9)[:, None, :]
    for repeat in range(ITERS):
        if repeat == 0:
            padded = padded_2(shaft_first, (("ply", 1),), 1)
        else:
            rounded = moved.astype(jnp.bfloat16)[:, None, :]
            padded = padded_2(rounded, (("shaft", 2), ("ply", 1)), 1)
        neighbours = jnp.zeros((slots,) + moved.shape, jnp.bfloat16)
        for code_index in range(9):
            shifted = padded[:, code_index // 3, code_index % 3 : code_index % 3 + blocks]
            neighbours = jnp.where(codes == code_index, shifted[None], neighbours)
        product = stiffness.astype(jnp.float32) * neighbours.astype(jnp.float32)[:, None, :, :]
        force = jnp.sum(product, axis=(0, 2)) + jnp.dot(
            strain_map.T, history, precision=lax.Precision.HIGHEST
        )
        speeds = speeds + time_step * (scaling * (forcing - force))
        advanced = moved + time_step * speeds
        history = decay * history + jnp.dot(
            strain_map, advanced - moved, precision=lax.Precision.HIGHEST
        )
        moved = advanced
    return (moved[:, None, :], speeds[:, None, :], history[:, None, :])


def solution(mesh):
    in_specs = (
        P(None, "ply", "shaft"),
        P(None, "ply", "shaft"),
        P(None, "ply", "shaft"),
        P(None, "ply", "shaft"),
        P(None, "ply", "shaft"),
        P("ply", "shaft"),
        P(None, None, None, ("shaft", "ply")),
        P(None, ("shaft", "ply")),
        P(None, ("shaft", "ply")),
        P(),
        P(("shaft", "ply"), None, None),
        P(("shaft", "ply"), None, None),
        P(("shaft", "ply"), None),
    )
    out_specs = (P(None, "ply", "shaft"), P(None, "ply", "shaft"), P(None, "ply", "shaft"))
    return jax.shard_map(
        on_device, mesh=mesh, in_specs=in_specs, out_specs=out_specs, check_vma=False
    )
```

```python
import jax
import jax.numpy as jnp
from jax import lax
from jax.experimental import pallas as pl
from jax.experimental.pallas import tpu as pltpu
from jax.sharding import PartitionSpec as P

ITERS = 4
ROWS = 8


time_step = 0.25


def padded_2(value, sides, width):
    for axis, dim in sides:
        size, length = (lax.axis_size(axis), value.shape[dim])
        up = [(i, (i + 1) % size) for i in range(size - 1)]
        down = [(j, i) for i, j in up]
        last = lax.slice_in_dim(value, length - width, length, axis=dim)
        first = lax.slice_in_dim(value, 0, width, axis=dim)
        before = lax.ppermute(last, axis, up)
        after = lax.ppermute(first, axis, down)
        value = jnp.concatenate([before, value, after], axis=dim)
    return value


def neighbour_exchange(axis, lower_bound, upper_bound):
    size = lax.axis_size(axis)
    up = [(i, i + 1) for i in range(size - 1)]
    down = [(i + 1, i) for i in range(size - 1)]
    from_lower = lax.ppermute(upper_bound, axis, up)
    from_higher = lax.ppermute(lower_bound, axis, down)
    return from_lower, from_higher


def gather_kernel(s_ref, lo_ref, hi_ref, out_lo_ref, out_hi_ref):
    width = lo_ref.shape[0]
    pick = jnp.concatenate([lo_ref[...], hi_ref[...]], 0)
    picked = lax.dot_general(
        pick, s_ref[0], (((1,), (1,)), ((), ())), preferred_element_type=jnp.float32
    )
    out_lo_ref[0] = picked[:width].astype(out_lo_ref.dtype)
    out_hi_ref[0] = picked[width:].astype(out_hi_ref.dtype)


def gather_leaving(stiffness, pick_lo, pick_hi):
    slots, depth, blocks = stiffness.shape
    width = pick_lo.shape[0]
    out = jax.ShapeDtypeStruct((slots, width, depth), stiffness.dtype)
    return pl.pallas_call(
        gather_kernel,
        grid=(slots,),
        in_specs=[
            pl.BlockSpec((1, depth, blocks), lambda k: (k, 0, 0)),
            pl.BlockSpec((width, blocks), lambda k: (0, 0)),
            pl.BlockSpec((width, blocks), lambda k: (0, 0)),
        ],
        out_specs=[
            pl.BlockSpec((1, width, depth), lambda k: (k, 0, 0)),
            pl.BlockSpec((1, width, depth), lambda k: (k, 0, 0)),
        ],
        out_shape=[out, out],
    )(stiffness, pick_lo, pick_hi)


def merge_kernel(s_ref, lo_ref, hi_ref, place_lo_ref, place_hi_ref, arrival_ref, out_ref):
    arrived = jnp.concatenate([lo_ref[0], hi_ref[0]], 0)
    place = jnp.concatenate([place_lo_ref[...], place_hi_ref[...]], 0)
    placed = jnp.dot(arrived.T, place, preferred_element_type=jnp.float32)
    placed = placed.astype(out_ref.dtype).reshape(s_ref.shape[1:])
    out_ref[0] = jnp.where(arrival_ref[...] > 0, placed, s_ref[0])


def merge_arrived(stiffness, arrived_lo, arrived_hi, place_lo, place_hi, arrival):
    slots, rows_i, rows_j, blocks = stiffness.shape
    depth = rows_i * rows_j
    width = arrived_lo.shape[1]
    return pl.pallas_call(
        merge_kernel,
        grid=(slots,),
        in_specs=[
            pl.BlockSpec((1, rows_i, rows_j, blocks), lambda k: (k, 0, 0, 0)),
            pl.BlockSpec((1, width, depth), lambda k: (k, 0, 0)),
            pl.BlockSpec((1, width, depth), lambda k: (k, 0, 0)),
            pl.BlockSpec((width, blocks), lambda k: (0, 0)),
            pl.BlockSpec((width, blocks), lambda k: (0, 0)),
            pl.BlockSpec((1, blocks), lambda k: (0, 0)),
        ],
        out_specs=pl.BlockSpec((1, rows_i, rows_j, blocks), lambda k: (k, 0, 0, 0)),
        out_shape=jax.ShapeDtypeStruct(stiffness.shape, stiffness.dtype),
    )(stiffness, arrived_lo, arrived_hi, place_lo, place_hi, arrival)


def force_kernel(s_ref, n_ref, out_ref):
    slots, rows = s_ref.shape[:2]
    for row in range(rows):
        acc = s_ref[0, row].astype(jnp.float32) * n_ref[0]
        for slot_index in range(1, slots):
            acc = acc + s_ref[slot_index, row].astype(jnp.float32) * n_ref[slot_index]
        out_ref[pl.ds(row, 1), :] = jnp.sum(acc, axis=0, keepdims=True)


def block_force(stiffness, neighbours):
    slots, rows_i, rows_j, blocks = stiffness.shape
    return pl.pallas_call(
        force_kernel,
        grid=(rows_i // ROWS,),
        in_specs=[
            pl.BlockSpec((slots, ROWS, rows_j, blocks), lambda i: (0, i, 0, 0)),
            pl.BlockSpec((slots, rows_j, blocks), lambda i: (0, 0, 0)),
        ],
        out_specs=pl.BlockSpec((ROWS, blocks), lambda i: (i, 0)),
        out_shape=jax.ShapeDtypeStruct((rows_i, blocks), jnp.float32),
        cost_estimate=pl.CostEstimate(
            flops=2 * slots * rows_i * rows_j * blocks,
            bytes_accessed=stiffness.size * 2 + neighbours.size * 4 + rows_i * blocks * 4,
            transcendentals=0,
        ),
    )(stiffness, neighbours)


def on_device(
    displacement,
    velocity,
    external,
    mass_inverse,
    pattern,
    coupled,
    stiffness_old,
    history_old,
    decay_old,
    strain_map,
    send_slot,
    arrive_place,
    arrive_count,
):
    blocks = displacement.shape[-1]
    capacity = send_slot.shape[2]
    slots = stiffness_old.shape[0]
    lanes = jnp.arange(blocks, dtype=jnp.int32)

    slots, rows_i, rows_j, _ = stiffness_old.shape
    stiff_flat = stiffness_old.reshape(slots, rows_i * rows_j, blocks)
    leave_lo = (send_slot[0, 0][:, None] == lanes[None, :]).astype(jnp.bfloat16)
    leave_hi = (send_slot[0, 1][:, None] == lanes[None, :]).astype(jnp.bfloat16)
    stiff_to_lower, stiff_to_higher = gather_leaving(stiff_flat, leave_lo, leave_hi)
    outgoing = send_slot[0].reshape(-1)
    moving_state = jnp.concatenate(
        [jnp.take(history_old, outgoing, axis=1), jnp.take(decay_old, outgoing, axis=1)], 0
    )
    high = lax.reduce_precision(moving_state, exponent_bits=8, mantissa_bits=7)
    rest = moving_state - high
    middle = lax.reduce_precision(rest, exponent_bits=8, mantissa_bits=7)
    low = rest - middle
    pieces = jnp.concatenate([high, middle, low], 0).astype(jnp.bfloat16).T
    pieces = jnp.pad(pieces, ((0, 0), (0, rows_i * rows_j - pieces.shape[1])))
    send_lower = jnp.concatenate([stiff_to_lower, pieces[None, :capacity]], 0)
    send_higher = jnp.concatenate([stiff_to_higher, pieces[None, capacity:]], 0)
    recv_lower, recv_higher = neighbour_exchange("shaft", send_lower, send_higher)
    stiff_lower, stiff_higher = recv_lower[:slots], recv_higher[:slots]
    state_parts = jnp.concatenate([recv_lower[slots], recv_higher[slots]], 0).T.astype(jnp.float32)
    state_count = moving_state.shape[0]
    state_arrived = (
        state_parts[:state_count]
        + state_parts[state_count : 2 * state_count]
        + state_parts[2 * state_count : 3 * state_count]
    )

    count_live = jnp.arange(capacity, dtype=jnp.int32)[None, :] < arrive_count[0][:, None]
    place_lo = (arrive_place[0, 0][:, None] == lanes[None, :]) & count_live[0][:, None]
    place_hi = (arrive_place[0, 1][:, None] == lanes[None, :]) & count_live[1][:, None]
    arrival = (jnp.any(place_lo, 0) | jnp.any(place_hi, 0)).astype(jnp.int32)[None, :]
    stiffness = merge_arrived(
        stiffness_old,
        stiff_lower,
        stiff_higher,
        place_lo.astype(jnp.bfloat16),
        place_hi.astype(jnp.bfloat16),
        arrival,
    )

    filled = count_live.reshape(-1)
    target = jnp.where(filled, arrive_place[0].reshape(-1), blocks)
    placing = (
        jnp.arange(blocks + 1, dtype=jnp.int32)
        .at[target]
        .set(blocks + jnp.arange(2 * capacity, dtype=jnp.int32))[:blocks]
    )
    depth = history_old.shape[0]
    history = jnp.take(jnp.concatenate([history_old, state_arrived[:depth]], 1), placing, axis=1)
    decay = jnp.take(jnp.concatenate([decay_old, state_arrived[depth:]], 1), placing, axis=1)

    moved = displacement[:, 0, :]
    speeds = velocity[:, 0, :]
    forcing = external[:, 0, :]
    scaling = mass_inverse[:, 0, :]
    live = jnp.arange(slots, dtype=jnp.int32)[:, None] < coupled[0][None, :]
    codes = jnp.where(live, pattern[:, 0, :], 9)[:, None, :]
    for repeat in range(ITERS):
        rounded = moved.astype(jnp.bfloat16)[:, None, :]
        padded = padded_2(rounded, (("shaft", 2), ("ply", 1)), 1)
        neighbours = jnp.zeros((slots,) + moved.shape, jnp.bfloat16)
        for code_index in range(9):
            shifted = padded[:, code_index // 3, code_index % 3 : code_index % 3 + blocks]
            neighbours = jnp.where(codes == code_index, shifted[None], neighbours)
        product = stiffness.astype(jnp.float32) * neighbours.astype(jnp.float32)[:, None, :, :]
        force = jnp.sum(product, axis=(0, 2)) + jnp.dot(
            strain_map.T, history, precision=lax.Precision.HIGHEST
        )
        speeds = speeds + time_step * (scaling * (forcing - force))
        advanced = moved + time_step * speeds
        history = decay * history + jnp.dot(
            strain_map, advanced - moved, precision=lax.Precision.HIGHEST
        )
        moved = advanced
    return (moved[:, None, :], speeds[:, None, :], history[:, None, :])


def solution(mesh):
    in_specs = (
        P(None, "ply", "shaft"),
        P(None, "ply", "shaft"),
        P(None, "ply", "shaft"),
        P(None, "ply", "shaft"),
        P(None, "ply", "shaft"),
        P("ply", "shaft"),
        P(None, None, None, ("shaft", "ply")),
        P(None, ("shaft", "ply")),
        P(None, ("shaft", "ply")),
        P(),
        P(("shaft", "ply"), None, None),
        P(("shaft", "ply"), None, None),
        P(("shaft", "ply"), None),
    )
    out_specs = (P(None, "ply", "shaft"), P(None, "ply", "shaft"), P(None, "ply", "shaft"))
    return jax.shard_map(
        on_device, mesh=mesh, in_specs=in_specs, out_specs=out_specs, check_vma=False
    )
```

```python
import jax
import jax.numpy as jnp
from jax import lax
from jax.experimental import pallas as pl
from jax.experimental.pallas import tpu as pltpu
from jax.sharding import PartitionSpec as P

ITERS = 4
ROWS = 8


time_step = 0.25


def padded_2(value, sides, width):
    for axis, dim in sides:
        size, length = (lax.axis_size(axis), value.shape[dim])
        up = [(i, (i + 1) % size) for i in range(size - 1)]
        down = [(j, i) for i, j in up]
        last = lax.slice_in_dim(value, length - width, length, axis=dim)
        first = lax.slice_in_dim(value, 0, width, axis=dim)
        before = lax.ppermute(last, axis, up)
        after = lax.ppermute(first, axis, down)
        value = jnp.concatenate([before, value, after], axis=dim)
    return value


def neighbour_exchange(axis, lower_bound, upper_bound):
    size = lax.axis_size(axis)
    up = [(i, i + 1) for i in range(size - 1)]
    down = [(i + 1, i) for i in range(size - 1)]
    from_lower = lax.ppermute(upper_bound, axis, up)
    from_higher = lax.ppermute(lower_bound, axis, down)
    return from_lower, from_higher


def gather_kernel(s_ref, pick_ref, out_lo_ref, out_hi_ref):
    width = out_lo_ref.shape[1]
    picked = lax.dot_general(
        pick_ref[...], s_ref[0], (((1,), (1,)), ((), ())), preferred_element_type=jnp.float32
    )
    out_lo_ref[0] = picked[:width].astype(out_lo_ref.dtype)
    out_hi_ref[0] = picked[width:].astype(out_hi_ref.dtype)


def gather_leaving(stiffness, pick):
    slots, depth, blocks = stiffness.shape
    width = pick.shape[0] // 2
    out = jax.ShapeDtypeStruct((slots, width, depth), stiffness.dtype)
    return pl.pallas_call(
        gather_kernel,
        grid=(slots,),
        in_specs=[
            pl.BlockSpec((1, depth, blocks), lambda k: (k, 0, 0)),
            pl.BlockSpec((2 * width, blocks), lambda k: (0, 0)),
        ],
        out_specs=[
            pl.BlockSpec((1, width, depth), lambda k: (k, 0, 0)),
            pl.BlockSpec((1, width, depth), lambda k: (k, 0, 0)),
        ],
        out_shape=[out, out],
    )(stiffness, pick)


def merge_kernel(s_ref, lo_ref, hi_ref, place_lo_ref, place_hi_ref, arrival_ref, out_ref):
    arrived = jnp.concatenate([lo_ref[0], hi_ref[0]], 0)
    place = jnp.concatenate([place_lo_ref[...], place_hi_ref[...]], 0)
    placed = jnp.dot(arrived.T, place, preferred_element_type=jnp.float32)
    placed = placed.astype(out_ref.dtype).reshape(s_ref.shape[1:])
    out_ref[0] = jnp.where(arrival_ref[...] > 0, placed, s_ref[0])


def merge_arrived(stiffness, arrived_lo, arrived_hi, place_lo, place_hi, arrival):
    slots, rows_i, rows_j, blocks = stiffness.shape
    depth = rows_i * rows_j
    width = arrived_lo.shape[1]
    return pl.pallas_call(
        merge_kernel,
        grid=(slots,),
        in_specs=[
            pl.BlockSpec((1, rows_i, rows_j, blocks), lambda k: (k, 0, 0, 0)),
            pl.BlockSpec((1, width, depth), lambda k: (k, 0, 0)),
            pl.BlockSpec((1, width, depth), lambda k: (k, 0, 0)),
            pl.BlockSpec((width, blocks), lambda k: (0, 0)),
            pl.BlockSpec((width, blocks), lambda k: (0, 0)),
            pl.BlockSpec((1, blocks), lambda k: (0, 0)),
        ],
        out_specs=pl.BlockSpec((1, rows_i, rows_j, blocks), lambda k: (k, 0, 0, 0)),
        out_shape=jax.ShapeDtypeStruct(stiffness.shape, stiffness.dtype),
    )(stiffness, arrived_lo, arrived_hi, place_lo, place_hi, arrival)


def force_kernel(s_ref, n_ref, out_ref):
    slots, rows = s_ref.shape[:2]
    for row in range(rows):
        acc = s_ref[0, row].astype(jnp.float32) * n_ref[0]
        for slot_index in range(1, slots):
            acc = acc + s_ref[slot_index, row].astype(jnp.float32) * n_ref[slot_index]
        out_ref[pl.ds(row, 1), :] = jnp.sum(acc, axis=0, keepdims=True)


def block_force(stiffness, neighbours):
    slots, rows_i, rows_j, blocks = stiffness.shape
    return pl.pallas_call(
        force_kernel,
        grid=(rows_i // ROWS,),
        in_specs=[
            pl.BlockSpec((slots, ROWS, rows_j, blocks), lambda i: (0, i, 0, 0)),
            pl.BlockSpec((slots, rows_j, blocks), lambda i: (0, 0, 0)),
        ],
        out_specs=pl.BlockSpec((ROWS, blocks), lambda i: (i, 0)),
        out_shape=jax.ShapeDtypeStruct((rows_i, blocks), jnp.float32),
        cost_estimate=pl.CostEstimate(
            flops=2 * slots * rows_i * rows_j * blocks,
            bytes_accessed=stiffness.size * 2 + neighbours.size * 4 + rows_i * blocks * 4,
            transcendentals=0,
        ),
    )(stiffness, neighbours)


def on_device(
    displacement,
    velocity,
    external,
    mass_inverse,
    pattern,
    coupled,
    stiffness_old,
    history_old,
    decay_old,
    strain_map,
    send_slot,
    arrive_place,
    arrive_count,
):
    blocks = displacement.shape[-1]
    capacity = send_slot.shape[2]
    slots = stiffness_old.shape[0]
    lanes = jnp.arange(blocks, dtype=jnp.int32)

    slots, rows_i, rows_j, _ = stiffness_old.shape
    stiff_flat = stiffness_old.reshape(slots, rows_i * rows_j, blocks)
    leaving = (send_slot[0].reshape(-1)[:, None] == lanes[None, :]).astype(jnp.bfloat16)
    stiff_to_lower, stiff_to_higher = gather_leaving(stiff_flat, leaving)
    stiff_lower, stiff_higher = neighbour_exchange("shaft", stiff_to_lower, stiff_to_higher)

    count_live = jnp.arange(capacity, dtype=jnp.int32)[None, :] < arrive_count[0][:, None]
    place_lo = (arrive_place[0, 0][:, None] == lanes[None, :]) & count_live[0][:, None]
    place_hi = (arrive_place[0, 1][:, None] == lanes[None, :]) & count_live[1][:, None]
    arrival = (jnp.any(place_lo, 0) | jnp.any(place_hi, 0)).astype(jnp.int32)[None, :]
    stiffness = merge_arrived(
        stiffness_old,
        stiff_lower,
        stiff_higher,
        place_lo.astype(jnp.bfloat16),
        place_hi.astype(jnp.bfloat16),
        arrival,
    )

    outgoing = send_slot[0].reshape(-1)
    filled = count_live.reshape(-1)
    target = jnp.where(filled, arrive_place[0].reshape(-1), blocks)
    placing = (
        jnp.arange(blocks + 1, dtype=jnp.int32)
        .at[target]
        .set(blocks + jnp.arange(2 * capacity, dtype=jnp.int32))[:blocks]
    )
    moving_state = jnp.concatenate(
        [jnp.take(history_old, outgoing, axis=1), jnp.take(decay_old, outgoing, axis=1)], 0
    )
    state_lower, state_higher = neighbour_exchange(
        "shaft", moving_state[:, :capacity], moving_state[:, capacity:]
    )
    state_arrived = jnp.concatenate([state_lower, state_higher], 1)
    depth = history_old.shape[0]
    history = jnp.take(jnp.concatenate([history_old, state_arrived[:depth]], 1), placing, axis=1)
    decay = jnp.take(jnp.concatenate([decay_old, state_arrived[depth:]], 1), placing, axis=1)

    moved = displacement[:, 0, :]
    speeds = velocity[:, 0, :]
    forcing = external[:, 0, :]
    scaling = mass_inverse[:, 0, :]
    live = jnp.arange(slots, dtype=jnp.int32)[:, None] < coupled[0][None, :]
    codes = jnp.where(live, pattern[:, 0, :], 9)[:, None, :]
    for repeat in range(ITERS):
        rounded = moved.astype(jnp.bfloat16)[:, None, :]
        padded = padded_2(rounded, (("shaft", 2), ("ply", 1)), 1)
        neighbours = jnp.zeros((slots,) + moved.shape, jnp.bfloat16)
        for code_index in range(9):
            shifted = padded[:, code_index // 3, code_index % 3 : code_index % 3 + blocks]
            neighbours = jnp.where(codes == code_index, shifted[None], neighbours)
        product = stiffness.astype(jnp.float32) * neighbours.astype(jnp.float32)[:, None, :, :]
        force = jnp.sum(product, axis=(0, 2)) + jnp.dot(
            strain_map.T, history, precision=lax.Precision.HIGHEST
        )
        speeds = speeds + time_step * (scaling * (forcing - force))
        advanced = moved + time_step * speeds
        history = decay * history + jnp.dot(
            strain_map, advanced - moved, precision=lax.Precision.HIGHEST
        )
        moved = advanced
    return (moved[:, None, :], speeds[:, None, :], history[:, None, :])


def solution(mesh):
    in_specs = (
        P(None, "ply", "shaft"),
        P(None, "ply", "shaft"),
        P(None, "ply", "shaft"),
        P(None, "ply", "shaft"),
        P(None, "ply", "shaft"),
        P("ply", "shaft"),
        P(None, None, None, ("shaft", "ply")),
        P(None, ("shaft", "ply")),
        P(None, ("shaft", "ply")),
        P(),
        P(("shaft", "ply"), None, None),
        P(("shaft", "ply"), None, None),
        P(("shaft", "ply"), None),
    )
    out_specs = (P(None, "ply", "shaft"), P(None, "ply", "shaft"), P(None, "ply", "shaft"))
    return jax.shard_map(
        on_device, mesh=mesh, in_specs=in_specs, out_specs=out_specs, check_vma=False
    )
```

```python
import jax
import jax.numpy as jnp
from jax import lax
from jax.experimental import pallas as pl
from jax.experimental.pallas import tpu as pltpu
from jax.sharding import PartitionSpec as P

ITERS = 4
ROWS = 8


time_step = 0.25


def padded_2(value, sides, width):
    for axis, dim in sides:
        size, length = (lax.axis_size(axis), value.shape[dim])
        up = [(i, (i + 1) % size) for i in range(size - 1)]
        down = [(j, i) for i, j in up]
        last = lax.slice_in_dim(value, length - width, length, axis=dim)
        first = lax.slice_in_dim(value, 0, width, axis=dim)
        before = lax.ppermute(last, axis, up)
        after = lax.ppermute(first, axis, down)
        value = jnp.concatenate([before, value, after], axis=dim)
    return value


def neighbour_exchange(axis, lower_bound, upper_bound):
    size = lax.axis_size(axis)
    up = [(i, i + 1) for i in range(size - 1)]
    down = [(i + 1, i) for i in range(size - 1)]
    from_lower = lax.ppermute(upper_bound, axis, up)
    from_higher = lax.ppermute(lower_bound, axis, down)
    return from_lower, from_higher


def gather_kernel(s_ref, lo_ref, hi_ref, out_lo_ref, out_hi_ref):
    width = lo_ref.shape[0]
    pick = jnp.concatenate([lo_ref[...], hi_ref[...]], 0)
    picked = lax.dot_general(
        pick, s_ref[0], (((1,), (1,)), ((), ())), preferred_element_type=jnp.float32
    )
    out_lo_ref[0] = picked[:width].astype(out_lo_ref.dtype)
    out_hi_ref[0] = picked[width:].astype(out_hi_ref.dtype)


def gather_leaving(stiffness, pick_lo, pick_hi):
    slots, depth, blocks = stiffness.shape
    width = pick_lo.shape[0]
    out = jax.ShapeDtypeStruct((slots, width, depth), stiffness.dtype)
    return pl.pallas_call(
        gather_kernel,
        grid=(slots,),
        in_specs=[
            pl.BlockSpec((1, depth, blocks), lambda k: (k, 0, 0)),
            pl.BlockSpec((width, blocks), lambda k: (0, 0)),
            pl.BlockSpec((width, blocks), lambda k: (0, 0)),
        ],
        out_specs=[
            pl.BlockSpec((1, width, depth), lambda k: (k, 0, 0)),
            pl.BlockSpec((1, width, depth), lambda k: (k, 0, 0)),
        ],
        out_shape=[out, out],
    )(stiffness, pick_lo, pick_hi)


def merge_kernel(s_ref, lo_ref, hi_ref, place_lo_ref, place_hi_ref, arrival_ref, out_ref):
    arrived = jnp.concatenate([lo_ref[0], hi_ref[0]], 0)
    place = jnp.concatenate([place_lo_ref[...], place_hi_ref[...]], 0)
    placed = jnp.dot(arrived.T, place, preferred_element_type=jnp.float32)
    placed = placed.astype(out_ref.dtype).reshape(s_ref.shape[1:])
    out_ref[0] = jnp.where(arrival_ref[...] > 0, placed, s_ref[0])


def merge_arrived(stiffness, arrived_lo, arrived_hi, place_lo, place_hi, arrival):
    slots, rows_i, rows_j, blocks = stiffness.shape
    depth = rows_i * rows_j
    width = arrived_lo.shape[1]
    return pl.pallas_call(
        merge_kernel,
        grid=(slots,),
        in_specs=[
            pl.BlockSpec((1, rows_i, rows_j, blocks), lambda k: (k, 0, 0, 0)),
            pl.BlockSpec((1, width, depth), lambda k: (k, 0, 0)),
            pl.BlockSpec((1, width, depth), lambda k: (k, 0, 0)),
            pl.BlockSpec((width, blocks), lambda k: (0, 0)),
            pl.BlockSpec((width, blocks), lambda k: (0, 0)),
            pl.BlockSpec((1, blocks), lambda k: (0, 0)),
        ],
        out_specs=pl.BlockSpec((1, rows_i, rows_j, blocks), lambda k: (k, 0, 0, 0)),
        out_shape=jax.ShapeDtypeStruct(stiffness.shape, stiffness.dtype),
    )(stiffness, arrived_lo, arrived_hi, place_lo, place_hi, arrival)


def force_kernel(s_ref, n_ref, out_ref):
    slots, rows = s_ref.shape[:2]
    for row in range(rows):
        acc = s_ref[0, row].astype(jnp.float32) * n_ref[0]
        for slot_index in range(1, slots):
            acc = acc + s_ref[slot_index, row].astype(jnp.float32) * n_ref[slot_index]
        out_ref[pl.ds(row, 1), :] = jnp.sum(acc, axis=0, keepdims=True)


def block_force(stiffness, neighbours):
    slots, rows_i, rows_j, blocks = stiffness.shape
    return pl.pallas_call(
        force_kernel,
        grid=(rows_i // ROWS,),
        in_specs=[
            pl.BlockSpec((slots, ROWS, rows_j, blocks), lambda i: (0, i, 0, 0)),
            pl.BlockSpec((slots, rows_j, blocks), lambda i: (0, 0, 0)),
        ],
        out_specs=pl.BlockSpec((ROWS, blocks), lambda i: (i, 0)),
        out_shape=jax.ShapeDtypeStruct((rows_i, blocks), jnp.float32),
        cost_estimate=pl.CostEstimate(
            flops=2 * slots * rows_i * rows_j * blocks,
            bytes_accessed=stiffness.size * 2 + neighbours.size * 4 + rows_i * blocks * 4,
            transcendentals=0,
        ),
    )(stiffness, neighbours)


def on_device(
    displacement,
    velocity,
    external,
    mass_inverse,
    pattern,
    coupled,
    stiffness_old,
    history_old,
    decay_old,
    strain_map,
    send_slot,
    arrive_place,
    arrive_count,
):
    blocks = displacement.shape[-1]
    capacity = send_slot.shape[2]
    slots = stiffness_old.shape[0]
    lanes = jnp.arange(blocks, dtype=jnp.int32)

    slots, rows_i, rows_j, _ = stiffness_old.shape
    stiff_flat = stiffness_old.reshape(slots, rows_i * rows_j, blocks)
    leave_lo = (send_slot[0, 0][:, None] == lanes[None, :]).astype(jnp.bfloat16)
    leave_hi = (send_slot[0, 1][:, None] == lanes[None, :]).astype(jnp.bfloat16)
    stiff_to_lower, stiff_to_higher = gather_leaving(stiff_flat, leave_lo, leave_hi)
    stiff_lower, stiff_higher = neighbour_exchange("shaft", stiff_to_lower, stiff_to_higher)

    count_live = jnp.arange(capacity, dtype=jnp.int32)[None, :] < arrive_count[0][:, None]
    place_lo = (arrive_place[0, 0][:, None] == lanes[None, :]) & count_live[0][:, None]
    place_hi = (arrive_place[0, 1][:, None] == lanes[None, :]) & count_live[1][:, None]
    arrival = (jnp.any(place_lo, 0) | jnp.any(place_hi, 0)).astype(jnp.int32)[None, :]
    stiffness = merge_arrived(
        stiffness_old,
        stiff_lower,
        stiff_higher,
        place_lo.astype(jnp.bfloat16),
        place_hi.astype(jnp.bfloat16),
        arrival,
    )

    outgoing = send_slot[0].reshape(-1)
    filled = count_live.reshape(-1)
    target = jnp.where(filled, arrive_place[0].reshape(-1), blocks)
    placing = (
        jnp.arange(blocks + 1, dtype=jnp.int32)
        .at[target]
        .set(blocks + jnp.arange(2 * capacity, dtype=jnp.int32))[:blocks]
    )
    moving_state = jnp.concatenate(
        [jnp.take(history_old, outgoing, axis=1), jnp.take(decay_old, outgoing, axis=1)], 0
    )
    state_lower, state_higher = neighbour_exchange(
        "shaft", moving_state[:, :capacity], moving_state[:, capacity:]
    )
    state_arrived = jnp.concatenate([state_lower, state_higher], 1)
    depth = history_old.shape[0]
    history = jnp.take(jnp.concatenate([history_old, state_arrived[:depth]], 1), placing, axis=1)
    decay = jnp.take(jnp.concatenate([decay_old, state_arrived[depth:]], 1), placing, axis=1)

    moved = displacement[:, 0, :]
    speeds = velocity[:, 0, :]
    forcing = external[:, 0, :]
    scaling = mass_inverse[:, 0, :]
    live = jnp.arange(slots, dtype=jnp.int32)[:, None] < coupled[0][None, :]
    codes = jnp.where(live, pattern[:, 0, :], 9)[:, None, :]
    for repeat in range(ITERS):
        rounded = moved.astype(jnp.bfloat16)[:, None, :]
        padded = padded_2(rounded, (("ply", 1), ("shaft", 2)), 1)
        neighbours = jnp.zeros((slots,) + moved.shape, jnp.bfloat16)
        for code_index in range(9):
            shifted = padded[:, code_index // 3, code_index % 3 : code_index % 3 + blocks]
            neighbours = jnp.where(codes == code_index, shifted[None], neighbours)
        product = stiffness.astype(jnp.float32) * neighbours.astype(jnp.float32)[:, None, :, :]
        force = jnp.sum(product, axis=(0, 2)) + jnp.dot(
            strain_map.T, history, precision=lax.Precision.HIGHEST
        )
        speeds = speeds + time_step * (scaling * (forcing - force))
        advanced = moved + time_step * speeds
        history = decay * history + jnp.dot(
            strain_map, advanced - moved, precision=lax.Precision.HIGHEST
        )
        moved = advanced
    return (moved[:, None, :], speeds[:, None, :], history[:, None, :])


def solution(mesh):
    in_specs = (
        P(None, "ply", "shaft"),
        P(None, "ply", "shaft"),
        P(None, "ply", "shaft"),
        P(None, "ply", "shaft"),
        P(None, "ply", "shaft"),
        P("ply", "shaft"),
        P(None, None, None, ("shaft", "ply")),
        P(None, ("shaft", "ply")),
        P(None, ("shaft", "ply")),
        P(),
        P(("shaft", "ply"), None, None),
        P(("shaft", "ply"), None, None),
        P(("shaft", "ply"), None),
    )
    out_specs = (P(None, "ply", "shaft"), P(None, "ply", "shaft"), P(None, "ply", "shaft"))
    return jax.shard_map(
        on_device, mesh=mesh, in_specs=in_specs, out_specs=out_specs, check_vma=False
    )
```
